32 devices in a mesh: dp: 2 (over x), mp: 16 (over z, y, core).
Axes of the slice: x: 2, y: 2, z: 4, core: 2. Of those that a mesh axis runs over, the one named last changes fastest.
Arguments:
- node_features: bfloat16 [512, 6144], P('mp', 'dp'), may hold values from -6 to 6
- weights_one: bfloat16 [1024, 512], replicated, may hold values from -0.25 to 0.25
- weights_two: bfloat16 [1024, 512], replicated, may hold values from -0.25 to 0.25
- neighbor_owner: int32 [6144, 8], P('dp'), may hold values from 0 to 15, all different within a row; in each aligned block of 192 rows (0 to 191, 192 to 383, ...) at most 144 rows name the same one
- neighbor_row: int32 [6144, 8], P('dp'), may hold values from 0 to 191
- neighbor_count: int32 [6144], P('dp'), may hold values from 4 to 8
- cotangent: bfloat16 [6144, 512], P(('dp', 'mp')), may hold values from -0.076171875 to 0.076171875
Outputs:
- node_output: bfloat16 [6144, 512], P(('dp', 'mp'))
- weight_grads: float32 [2048, 512], P(('dp', 'mp'))
The draws below stay inside these ranges and needn't reach their ends.
Inputs may be any that keep to these rules, and one draw needn't show every extreme that they name: `neighbor_owner`: each row names 8 different owners; among the rows of one device (aligned blocks of 192 rows) no owner is named more than 144 times, and in some block one owner exactly 144 times. Slots k >= neighbor_count[r] are padding and carry no edge.
All inputs are finite; a program needn't handle non-finite values.
Results may differ from the reference program's by a relative error of at most 0.0052.
Values may be sent and summed in bfloat16 or wider, within the bound.
No kernel may reach another device: no remote copies, remote signals or barrier semaphores. Data moves between devices by JAX's collectives and lax.ppermute only.
A program may use at most 64 MiB of HBM per device.

```python
import math
import jax
import jax.numpy as jnp
import numpy as np
from jax import lax

F = 512
H = 512
K = 8
NODE_DEV = 192
NODES = 3072
ROWS = 6144
CAP = 144
N_DP = 2
N_MP = 16


def plant(values, own_key, least, high):
    spot = [jax.random.randint(jax.random.fold_in(own_key, axis), (), 0, length) for axis, length in enumerate(values.shape)]
    longest = values.shape.index(max(values.shape))
    neighbour = spot[:longest] + [(spot[longest] + 1) % values.shape[longest]] + spot[longest + 1:]
    return values.at[tuple(spot)].set(least).at[tuple(neighbour)].set(high)


def with_spikes(entries, stream_key, source, target, parts, factor):
    def block_of(position):
        return (jnp.arange(entries.shape[position]) // (entries.shape[position] // parts)).reshape((-1,) + (1,) * (entries.ndim - 1 - position))

    one_side = jax.random.permutation(stream_key, parts)[block_of(target)]
    second = (block_of(target) + parts // 2) % parts
    return jnp.where((block_of(source) == one_side) | (block_of(source) == second), factor * entries, entries)


def block_scale(rng, dims, pieces, smallest, top_value):
    loudness, own = 1.0, jax.random.fold_in(rng, 6)
    for dim, shards_of in pieces:
        heights = jnp.exp(jax.random.uniform(jax.random.fold_in(own, dim), (shards_of,), jnp.float32, smallest / len(pieces), top_value / len(pieces)))
        loudness = loudness * jnp.repeat(heights, dims[dim] // shards_of).reshape([-1 if axis == dim else 1 for axis in range(len(dims))])
    return loudness


def assign_block(stream_key, own, number, rows, count, top, most, skew):
    ranking = jax.random.permutation(stream_key, count)
    packed, usual = portions_of(count, rows * top, most, skew, True), portions_of(count, rows * top, most, skew, False)
    places = jnp.arange(count)

    def named(tallies, offset_by):
        used = int((tallies > 0).sum())
        fixed = max(1, used // 4)
        moved = fixed + (places - fixed + offset_by * (used - fixed)) % max(1, count - fixed)
        return jnp.zeros((count,), jnp.int32).at[ranking[jnp.where(places < fixed, places, moved)]].set(jnp.asarray(tallies, jnp.int32))

    tallies = jnp.where(number % 4 == 0, named(packed, number // 4), named(usual, number - number // 4 - 1))
    mixed = jax.random.permutation(jax.random.fold_in(own, 3), count)
    donor, sink = mixed[0:count // 2 * 2:2], mixed[1:count // 2 * 2:2]
    room = jnp.minimum(tallies[donor] - 1, most - tallies[sink]) // 2
    room = jnp.where((donor == ranking[0]) | (sink == ranking[0]) | (tallies[sink] == 0), 0, jnp.maximum(room, 0))
    moved = jax.random.randint(jax.random.fold_in(own, 4), (count // 2,), 0, 1 << 20) % (room + 1)
    tallies = tallies.at[donor].add(-moved).at[sink].add(moved)
    members = jnp.searchsorted(jnp.cumsum(tallies), jnp.arange(rows * top), side="right").astype(jnp.int32)
    grid = members.reshape(top, rows).T
    grid = grid[jax.random.permutation(jax.random.fold_in(own, 1), rows)]
    offset_by = jax.random.randint(jax.random.fold_in(own, 2), (rows, 1), 0, top)
    return jnp.take_along_axis(grid, (jnp.arange(top)[None, :] + offset_by) % top, axis=1)


def portions_of(amount, total, limit, lean, full):
    loads = [(1 << 20) // math.isqrt(rank ** lean) + 1 for rank in range(1, amount + 1)]
    largest = limit if full else min(limit, max(-(-total // amount), total * loads[0] // sum(loads)))
    least = 1 if total - largest >= amount - 1 else 0
    given, spare = [largest] + [least] * (amount - 1), total - largest - least * (amount - 1)
    while spare > 0:
        movable = [i for i in range(1, amount) if given[i] < largest] or [i for i in range(1, amount) if given[i] < limit]
        mass, budget = sum([loads[i] for i in movable]), spare
        for i in movable:
            extra = min(limit - given[i], max(1, budget * loads[i] // mass), spare)
            given[i] = given[i] + extra
            spare = spare - extra
    return np.array(given)


def scatter_about(own_key, extent, deviation, limit, cuts=(), kind=jnp.bfloat16):
    level = block_scale(own_key, extent, cuts, -0.22, 0.18) if cuts else 1.0
    array = jax.random.normal(own_key, extent, jnp.float32) * deviation * level
    return jnp.minimum(jnp.maximum(array, -limit), limit).astype(kind)


def bell_draw_with(own_key, extent, scale, reach, pieces, heavy, kind=jnp.bfloat16):
    drawn = scale * jax.random.normal(own_key, extent, jnp.float32)
    if pieces:
        drawn = drawn * block_scale(own_key, extent, pieces, -0.22, 0.18)
    return jnp.clip(with_spikes(drawn, jax.random.fold_in(own_key, 3), *heavy), -reach, reach).astype(kind)


def setup_inputs(seed: int = 0) -> dict:
    key_list = jax.random.split(jax.random.key(seed), 8)
    node_features = bell_draw_with(key_list[0], (F, ROWS), 1.0, 6.0, ((0, 16), (1, 2)), (1, 0, 16, 2.0))
    weights_one = scatter_about(key_list[1], (2 * F, H), F ** -0.5, 0.25)
    weights_two = scatter_about(key_list[2], (2 * H, H), H ** -0.5, 0.25)
    neighbor_owner_keys = jax.random.split(jax.random.fold_in(key_list[3], 1), ROWS // NODE_DEV)
    neighbor_owner_turns = jax.random.permutation(jax.random.fold_in(key_list[3], 3), ROWS // NODE_DEV)
    neighbor_owner = jax.vmap(lambda own, number: assign_block(jax.random.fold_in(key_list[3], 2), own, number, NODE_DEV, N_MP, K, CAP, 1))(neighbor_owner_keys, neighbor_owner_turns).reshape((ROWS, K))
    neighbor_row = plant(jax.random.randint(key_list[4], (ROWS, K), 0, NODE_DEV), jax.random.fold_in(key_list[4], 1), 0, NODE_DEV - 1).astype(jnp.int32)
    neighbor_count = plant(jax.random.randint(key_list[5], (ROWS,), K // 2, K + 1), jax.random.fold_in(key_list[5], 1), K // 2, K).astype(jnp.int32)
    cotangent = scatter_about(key_list[6], (ROWS, H), (2.0 * (N_DP * NODES) ** -0.5), 0.076171875, ((0, 32),))
    return dict(node_features=node_features, weights_one=weights_one, weights_two=weights_two, neighbor_owner=neighbor_owner, neighbor_row=neighbor_row, neighbor_count=neighbor_count, cotangent=cotangent)


def dot32(left, right):
    return jnp.dot(left.astype(jnp.float32), right.astype(jnp.float32), precision=lax.Precision.HIGHEST)


def column_mean(table, indices, live, inverse):
    total = jnp.zeros((table.shape[0], indices.shape[0]), jnp.float32)
    for slot_index in range(indices.shape[1]):
        picked = jnp.take(table, indices[:, slot_index], axis=1)
        kept = jnp.where(live[:, slot_index][None, :], picked, jnp.zeros_like(picked))
        total = total + kept.astype(jnp.float32)
    return (total * inverse[None, :]).astype(jnp.bfloat16)


def reference(node_features, weights_one, weights_two, neighbor_owner, neighbor_row, neighbor_count, cotangent):
    rows_all = neighbor_owner.shape[0]
    base_rows = (jnp.arange(rows_all, dtype=jnp.int32) // NODES) * NODES
    global_ids = (base_rows[:, None] + neighbor_owner * NODE_DEV + neighbor_row).astype(jnp.int32)
    live = jnp.arange(K, dtype=jnp.int32)[None, :] < neighbor_count[:, None]
    inverse = 1.0 / neighbor_count.astype(jnp.float32)
    agg_one = column_mean(node_features, global_ids, live, inverse).T
    rows_feat = node_features.T
    pre_one = dot32(rows_feat, weights_one[:F])
    pre_one = pre_one + dot32(agg_one, weights_one[F:])
    hidden_one = jax.nn.silu(pre_one).astype(jnp.bfloat16)
    agg_two = column_mean(hidden_one.T, global_ids, live, inverse).T
    node_output = dot32(hidden_one, weights_two[:H])
    node_output = (node_output + dot32(agg_two, weights_two[H:])).astype(jnp.bfloat16)
    down_self = dot32(cotangent, weights_two[:H].T)
    down_neigh = (dot32(cotangent, weights_two[H:].T) * inverse[:, None]).astype(jnp.bfloat16)
    neighbor_sum = jnp.zeros((rows_all, H), jnp.float32)
    for slot_index in range(K):
        kept = jnp.where(live[:, slot_index][:, None], down_neigh, jnp.zeros_like(down_neigh)).astype(jnp.float32)
        neighbor_sum = neighbor_sum.at[global_ids[:, slot_index]].add(kept)
    grad_hidden = down_self + neighbor_sum
    sigmoid = jax.nn.sigmoid(pre_one)
    grad_pre = (grad_hidden * sigmoid * (1.0 + pre_one * (1.0 - sigmoid))).astype(jnp.bfloat16)
    weight_grads = jnp.concatenate([
        dot32(node_features, grad_pre),
        dot32(agg_one.T, grad_pre),
        dot32(hidden_one.T, cotangent),
        dot32(agg_two.T, cotangent)], axis=0)
    return node_output, weight_grads
```

```python
import jax
import jax.numpy as jnp
from jax import lax
from jax.sharding import PartitionSpec as P


def column_mean(table, indices, live, inverse):
    total = jnp.zeros((table.shape[0], indices.shape[1]), jnp.float32)
    for slot_index in range(indices.shape[0]):
        picked = jnp.take(table, indices[slot_index], axis=1)
        kept = jnp.where(live[slot_index][None, :], picked, jnp.zeros_like(picked))
        total = total + kept.astype(jnp.float32)
    return (total * inverse[None, :]).astype(jnp.bfloat16)


def silu_slope(values):
    sigmoid = jax.nn.sigmoid(values)
    return sigmoid * (1.0 + values * (1.0 - sigmoid))


def contract(left, right, left_dim, right_dim):
    return lax.dot_general(
        left, right, (((left_dim,), (right_dim,)), ((), ())), preferred_element_type=jnp.float32
    )


def shards(
    node_features, weights_one, weights_two, neighbor_owner, neighbor_row, neighbor_count, cotangent
):
    devices = lax.axis_size("mp")
    own_index = lax.axis_index("mp")
    node_dev = cotangent.shape[0]
    all_nodes = neighbor_owner.shape[0]
    fanout = neighbor_owner.shape[1]
    feat_width = weights_one.shape[0] // 2
    hidden = weights_one.shape[1]
    capacity = 3 * node_dev * fanout // (2 * devices)
    live = lax.broadcasted_iota(jnp.int32, (all_nodes, fanout), 1) < neighbor_count[:, None]
    inverse_all = 1.0 / neighbor_count.astype(jnp.float32)

    owner_ids = lax.broadcasted_iota(jnp.int32, (devices, 1, 1), 0)
    match = (neighbor_owner[None, :, :] == owner_ids) & live[None, :, :]
    rowsel = jnp.max(jnp.where(match, neighbor_row[None, :, :], -1), axis=2)
    has = rowsel >= 0

    with jax.named_scope("layer_one_mean"):
        if all_nodes * all_nodes <= 4096 * 4096:
            row_ids = lax.broadcasted_iota(jnp.int32, (1, node_dev, 1), 1)
            adjacency = (rowsel[:, None, :] == row_ids).astype(jnp.bfloat16)
            adjacency = adjacency.reshape(devices * node_dev, all_nodes)
            summed = contract(node_features, adjacency, 1, 0)
            agg_one_cols = (summed * inverse_all[None, :]).astype(jnp.bfloat16)
        else:
            owner_slots = neighbor_owner.T
            global_ids = owner_slots * node_dev + neighbor_row.T
            agg_one_cols = column_mean(node_features, global_ids, live.T, inverse_all)

    own_feats, own_agg_one = (
        lax.all_to_all(node_features, "mp", split_axis=1, concat_axis=0, tiled=True),
        lax.all_to_all(agg_one_cols, "mp", split_axis=1, concat_axis=0, tiled=True),
    )
    pre_one = contract(weights_one[:feat_width], own_feats, 0, 0) + contract(
        weights_one[feat_width:], own_agg_one, 0, 0
    )
    hidden_one = jax.nn.silu(pre_one).astype(jnp.bfloat16)

    with jax.named_scope("slot_tables"):
        blocks = has.reshape(devices * devices, node_dev).astype(jnp.bfloat16)
        before = (
            lax.broadcasted_iota(jnp.int32, (node_dev, node_dev), 0)
            < lax.broadcasted_iota(jnp.int32, (node_dev, node_dev), 1)
        ).astype(jnp.bfloat16)
        ranks = contract(blocks, before, 1, 0).astype(jnp.int32).reshape(devices, devices, node_dev)
        has_blocks = has.reshape(devices, devices, node_dev)
        rows_blocks = rowsel.reshape(devices, devices, node_dev)
        cap_ids = lax.broadcasted_iota(jnp.int32, (1, capacity, 1), 1)
        own_rank = lax.dynamic_index_in_dim(ranks, own_index, 1, keepdims=False)
        own_has = lax.dynamic_index_in_dim(has_blocks, own_index, 1, keepdims=False)
        gathered = ((own_rank[:, None, :] == cap_ids) & own_has[:, None, :]).astype(jnp.bfloat16)
        gathered = gathered.reshape(devices * capacity, node_dev)
        req_rank = lax.dynamic_index_in_dim(ranks, own_index, 0, keepdims=False)
        req_has = lax.dynamic_index_in_dim(has_blocks, own_index, 0, keepdims=False)
        req_rows = lax.dynamic_index_in_dim(rows_blocks, own_index, 0, keepdims=False)
        pick = ((req_rank[:, None, :] == cap_ids) & req_has[:, None, :]).astype(jnp.bfloat16)
        row_ids = lax.broadcasted_iota(jnp.int32, (1, 1, node_dev), 2)
        which = (req_rows[:, :, None] == row_ids).astype(jnp.bfloat16)
        asked = lax.dot_general(
            pick, which, (((2,), (1,)), ((0,), (0,))), preferred_element_type=jnp.float32
        )
        asked = asked.astype(jnp.bfloat16).reshape(devices * capacity, node_dev)

    own_inverse = lax.dynamic_slice_in_dim(inverse_all, own_index * node_dev, node_dev, 0)
    outgoing = contract(hidden_one, asked, 1, 1).astype(jnp.bfloat16)
    incoming = lax.all_to_all(outgoing, "mp", split_axis=1, concat_axis=1, tiled=True)
    total = contract(incoming, gathered, 1, 0)
    agg_two = (total * own_inverse[None, :]).astype(jnp.bfloat16)
    self_two = weights_two[:hidden]
    neigh_two = weights_two[hidden:]
    node_output = (
        contract(hidden_one, self_two, 0, 0) + contract(agg_two, neigh_two, 0, 0)
    ).astype(jnp.bfloat16)
    down_self = contract(self_two, cotangent, 1, 1)
    down_neigh = (contract(neigh_two, cotangent, 1, 1) * own_inverse[None, :]).astype(jnp.bfloat16)
    outgoing_grad = contract(down_neigh, gathered, 1, 1).astype(jnp.bfloat16)
    incoming_grad = lax.all_to_all(outgoing_grad, "mp", split_axis=1, concat_axis=1, tiled=True)
    neighbor_sum = contract(incoming_grad, asked, 1, 0)
    grad_hidden = down_self + neighbor_sum
    grad_pre = (grad_hidden * silu_slope(pre_one)).astype(jnp.bfloat16)
    terms = jnp.concatenate(
        [
            contract(own_feats, grad_pre, 1, 1),
            contract(own_agg_one, grad_pre, 1, 1),
            contract(hidden_one, cotangent, 1, 0),
            contract(agg_two, cotangent, 1, 0),
        ],
        axis=0,
    )
    weight_grads = lax.psum_scatter(terms, ("dp", "mp"), scatter_dimension=0, tiled=True)
    return (node_output, weight_grads)


def solution(mesh):
    in_specs = (
        P("mp", "dp"),
        P(),
        P(),
        P("dp", None),
        P("dp", None),
        P("dp"),
        P(("dp", "mp"), None),
    )
    out_specs = (P(("dp", "mp"), None), P(("dp", "mp"), None))
    return jax.shard_map(shards, mesh=mesh, in_specs=in_specs, out_specs=out_specs, check_vma=False)
```

```python
import jax
import jax.numpy as jnp
from jax import lax
from jax.sharding import PartitionSpec as P


def column_mean(table, indices, live, inverse):
    total = jnp.zeros((table.shape[0], indices.shape[1]), jnp.float32)
    for slot_index in range(indices.shape[0]):
        picked = jnp.take(table, indices[slot_index], axis=1)
        kept = jnp.where(live[slot_index][None, :], picked, jnp.zeros_like(picked))
        total = total + kept.astype(jnp.float32)
    return (total * inverse[None, :]).astype(jnp.bfloat16)


def silu_slope(values):
    sigmoid = jax.nn.sigmoid(values)
    return sigmoid * (1.0 + values * (1.0 - sigmoid))


def contract(left, right, left_dim, right_dim):
    return lax.dot_general(
        left, right, (((left_dim,), (right_dim,)), ((), ())), preferred_element_type=jnp.float32
    )


def swap(values, axis, mask):
    size = lax.axis_size(axis)
    return lax.ppermute(values, axis, [(j, j ^ mask) for j in range(size)])


def halving_scatter(terms, order):
    n_mp = lax.axis_size("mp")
    top = n_mp.bit_length() - 1
    place = lax.axis_index("dp") * n_mp + lax.axis_index("mp")
    rows = terms.shape[0] // (2 * n_mp)
    bits = list(range(top, -1, -1))
    values = terms.reshape((2,) * (top + 1) + (rows, terms.shape[1]))
    for bit in order:
        position = bits.index(bit)
        mine = (place >> bit) & 1
        keep = lax.dynamic_index_in_dim(values, mine, position, keepdims=False)
        send = lax.dynamic_index_in_dim(values, 1 - mine, position, keepdims=False)
        got = swap(send, "dp", 1) if bit == top else swap(send, "mp", 1 << bit)
        values = keep + got
        bits.pop(position)
    return values.reshape(rows, terms.shape[1])


def shards(
    node_features, weights_one, weights_two, neighbor_owner, neighbor_row, neighbor_count, cotangent
):
    devices = lax.axis_size("mp")
    own_index = lax.axis_index("mp")
    node_dev = cotangent.shape[0]
    all_nodes = neighbor_owner.shape[0]
    fanout = neighbor_owner.shape[1]
    feat_width = weights_one.shape[0] // 2
    hidden = weights_one.shape[1]
    capacity = 3 * node_dev * fanout // (2 * devices)
    live = lax.broadcasted_iota(jnp.int32, (all_nodes, fanout), 1) < neighbor_count[:, None]
    inverse_all = 1.0 / neighbor_count.astype(jnp.float32)

    owner_ids = lax.broadcasted_iota(jnp.int32, (devices, 1, 1), 0)
    match = (neighbor_owner[None, :, :] == owner_ids) & live[None, :, :]
    rowsel = jnp.max(jnp.where(match, neighbor_row[None, :, :], -1), axis=2)
    has = rowsel >= 0

    with jax.named_scope("layer_one_mean"):
        if all_nodes * all_nodes <= 4096 * 4096:
            row_ids = lax.broadcasted_iota(jnp.int32, (1, node_dev, 1), 1)
            adjacency = (rowsel[:, None, :] == row_ids).astype(jnp.bfloat16)
            adjacency = adjacency.reshape(devices * node_dev, all_nodes)
            summed = contract(node_features, adjacency, 1, 0)
            agg_one_cols = (summed * inverse_all[None, :]).astype(jnp.bfloat16)
        else:
            owner_slots = neighbor_owner.T
            global_ids = owner_slots * node_dev + neighbor_row.T
            agg_one_cols = column_mean(node_features, global_ids, live.T, inverse_all)

    own_feats, own_agg_one = (
        lax.all_to_all(node_features, "mp", split_axis=1, concat_axis=0, tiled=True),
        lax.all_to_all(agg_one_cols, "mp", split_axis=1, concat_axis=0, tiled=True),
    )
    pre_one = contract(weights_one[:feat_width], own_feats, 0, 0) + contract(
        weights_one[feat_width:], own_agg_one, 0, 0
    )
    hidden_one = jax.nn.silu(pre_one).astype(jnp.bfloat16)

    with jax.named_scope("slot_tables"):
        blocks = has.reshape(devices * devices, node_dev).astype(jnp.bfloat16)
        before = (
            lax.broadcasted_iota(jnp.int32, (node_dev, node_dev), 0)
            < lax.broadcasted_iota(jnp.int32, (node_dev, node_dev), 1)
        ).astype(jnp.bfloat16)
        ranks = contract(blocks, before, 1, 0).astype(jnp.int32).reshape(devices, devices, node_dev)
        has_blocks = has.reshape(devices, devices, node_dev)
        rows_blocks = rowsel.reshape(devices, devices, node_dev)
        cap_ids = lax.broadcasted_iota(jnp.int32, (1, capacity, 1), 1)
        own_rank = lax.dynamic_index_in_dim(ranks, own_index, 1, keepdims=False)
        own_has = lax.dynamic_index_in_dim(has_blocks, own_index, 1, keepdims=False)
        gathered = ((own_rank[:, None, :] == cap_ids) & own_has[:, None, :]).astype(jnp.bfloat16)
        gathered = gathered.reshape(devices * capacity, node_dev)
        req_rank = lax.dynamic_index_in_dim(ranks, own_index, 0, keepdims=False)
        req_has = lax.dynamic_index_in_dim(has_blocks, own_index, 0, keepdims=False)
        req_rows = lax.dynamic_index_in_dim(rows_blocks, own_index, 0, keepdims=False)
        pick = ((req_rank[:, None, :] == cap_ids) & req_has[:, None, :]).astype(jnp.bfloat16)
        row_ids = lax.broadcasted_iota(jnp.int32, (1, 1, node_dev), 2)
        which = (req_rows[:, :, None] == row_ids).astype(jnp.bfloat16)
        asked = lax.dot_general(
            pick, which, (((2,), (1,)), ((0,), (0,))), preferred_element_type=jnp.float32
        )
        asked = asked.astype(jnp.bfloat16).reshape(devices * capacity, node_dev)

    own_inverse = lax.dynamic_slice_in_dim(inverse_all, own_index * node_dev, node_dev, 0)
    outgoing = contract(hidden_one, asked, 1, 1).astype(jnp.bfloat16)
    incoming = lax.all_to_all(outgoing, "mp", split_axis=1, concat_axis=1, tiled=True)
    total = contract(incoming, gathered, 1, 0)
    agg_two = (total * own_inverse[None, :]).astype(jnp.bfloat16)
    self_two = weights_two[:hidden]
    neigh_two = weights_two[hidden:]
    node_output = (
        contract(hidden_one, self_two, 0, 0) + contract(agg_two, neigh_two, 0, 0)
    ).astype(jnp.bfloat16)
    down_self = contract(self_two, cotangent, 1, 1)
    down_neigh = (contract(neigh_two, cotangent, 1, 1) * own_inverse[None, :]).astype(jnp.bfloat16)
    outgoing_grad = contract(down_neigh, gathered, 1, 1).astype(jnp.bfloat16)
    incoming_grad = lax.all_to_all(outgoing_grad, "mp", split_axis=1, concat_axis=1, tiled=True)
    neighbor_sum = contract(incoming_grad, asked, 1, 0)
    grad_hidden = down_self + neighbor_sum
    grad_pre = (grad_hidden * silu_slope(pre_one)).astype(jnp.bfloat16)
    terms = jnp.concatenate(
        [
            contract(own_feats, grad_pre, 1, 1),
            contract(own_agg_one, grad_pre, 1, 1),
            contract(hidden_one, cotangent, 1, 0),
            contract(agg_two, cotangent, 1, 0),
        ],
        axis=0,
    )
    with jax.named_scope("weight_grad_sum"):
        if lax.axis_size("dp") == 2 and devices == 16:
            weight_grads = halving_scatter(terms, [0, 4, 1, 3, 2])
        else:
            weight_grads = lax.psum_scatter(terms, ("dp", "mp"), scatter_dimension=0, tiled=True)
    return (node_output, weight_grads)


def solution(mesh):
    in_specs = (
        P("mp", "dp"),
        P(),
        P(),
        P("dp", None),
        P("dp", None),
        P("dp"),
        P(("dp", "mp"), None),
    )
    out_specs = (P(("dp", "mp"), None), P(("dp", "mp"), None))
    return jax.shard_map(shards, mesh=mesh, in_specs=in_specs, out_specs=out_specs, check_vma=False)
```

```python
import jax
import jax.numpy as jnp
from jax import lax
from jax.sharding import PartitionSpec as P


def column_mean(table, indices, live, inverse):
    total = jnp.zeros((table.shape[0], indices.shape[1]), jnp.float32)
    for slot_index in range(indices.shape[0]):
        picked = jnp.take(table, indices[slot_index], axis=1)
        kept = jnp.where(live[slot_index][None, :], picked, jnp.zeros_like(picked))
        total = total + kept.astype(jnp.float32)
    return (total * inverse[None, :]).astype(jnp.bfloat16)


def silu_slope(values):
    sigmoid = jax.nn.sigmoid(values)
    return sigmoid * (1.0 + values * (1.0 - sigmoid))


def contract(left, right, left_dim, right_dim):
    return lax.dot_general(
        left, right, (((left_dim,), (right_dim,)), ((), ())), preferred_element_type=jnp.float32
    )


def swap(values, axis, mask):
    size = lax.axis_size(axis)
    return lax.ppermute(values, axis, [(j, j ^ mask) for j in range(size)])


def halving_scatter(terms, order):
    n_mp = lax.axis_size("mp")
    top = n_mp.bit_length() - 1
    place = lax.axis_index("dp") * n_mp + lax.axis_index("mp")
    rows = terms.shape[0] // (2 * n_mp)
    bits = list(range(top, -1, -1))
    values = terms.reshape((2,) * (top + 1) + (rows, terms.shape[1]))
    for bit in order:
        position = bits.index(bit)
        mine = (place >> bit) & 1
        keep = lax.dynamic_index_in_dim(values, mine, position, keepdims=False)
        send = lax.dynamic_index_in_dim(values, 1 - mine, position, keepdims=False)
        got = swap(send, "dp", 1) if bit == top else swap(send, "mp", 1 << bit)
        values = keep + got
        bits.pop(position)
    return values.reshape(rows, terms.shape[1])


def doubling_gather(rows, order):
    own = lax.axis_index("mp")
    current = rows
    for step, bit in enumerate(order):
        got = swap(current, "mp", 1 << bit)
        low = jnp.where((own >> bit) & 1 == 0, current, got)
        high = jnp.where((own >> bit) & 1 == 0, got, current)
        current = jnp.stack([low, high], axis=step)
    return current.reshape(-1, rows.shape[-1])


def shards(
    node_features, weights_one, weights_two, neighbor_owner, neighbor_row, neighbor_count, cotangent
):
    devices = lax.axis_size("mp")
    own_index = lax.axis_index("mp")
    node_dev = cotangent.shape[0]
    all_nodes = neighbor_owner.shape[0]
    fanout = neighbor_owner.shape[1]
    feat_width = weights_one.shape[0] // 2
    hidden = weights_one.shape[1]
    live = lax.broadcasted_iota(jnp.int32, (all_nodes, fanout), 1) < neighbor_count[:, None]
    inverse_all = 1.0 / neighbor_count.astype(jnp.float32)

    owner_ids = lax.broadcasted_iota(jnp.int32, (devices, 1, 1), 0)
    match = (neighbor_owner[None, :, :] == owner_ids) & live[None, :, :]
    rowsel = jnp.max(jnp.where(match, neighbor_row[None, :, :], -1), axis=2)

    with jax.named_scope("layer_one_mean"):
        if all_nodes * all_nodes <= 4096 * 4096:
            row_ids = lax.broadcasted_iota(jnp.int32, (1, node_dev, 1), 1)
            adjacency = (rowsel[:, None, :] == row_ids).astype(jnp.bfloat16)
            adjacency = adjacency.reshape(devices * node_dev, all_nodes)
            summed = contract(node_features, adjacency, 1, 0)
            agg_one_cols = (summed * inverse_all[None, :]).astype(jnp.bfloat16)
        else:
            owner_slots = neighbor_owner.T
            global_ids = owner_slots * node_dev + neighbor_row.T
            agg_one_cols = column_mean(node_features, global_ids, live.T, inverse_all)

    own_feats, own_agg_one = (
        lax.all_to_all(node_features, "mp", split_axis=1, concat_axis=0, tiled=True),
        lax.all_to_all(agg_one_cols, "mp", split_axis=1, concat_axis=0, tiled=True),
    )
    self_two = weights_two[:hidden]
    neigh_two = weights_two[hidden:]
    own_inverse = lax.dynamic_slice_in_dim(inverse_all, own_index * node_dev, node_dev, 0)
    order = list(range(devices.bit_length() - 2, -1, -1))

    with jax.named_scope("neighbor_tables"):
        row_ids = lax.broadcasted_iota(jnp.int32, (1, node_dev, 1), 1)
        own_sel = lax.dynamic_slice_in_dim(rowsel, own_index * node_dev, node_dev, 1)
        own_edges = (own_sel[:, None, :] == row_ids).astype(jnp.bfloat16)
        own_edges = own_edges.reshape(devices * node_dev, node_dev)
        mine_sel = lax.dynamic_index_in_dim(rowsel, own_index, 0, keepdims=False)
        named_by = (mine_sel[:, None] == row_ids.reshape(1, node_dev)).astype(jnp.bfloat16)

    down_neigh = (contract(cotangent, neigh_two, 1, 1) * own_inverse[:, None]).astype(jnp.bfloat16)
    down_all = doubling_gather(down_neigh, order)

    pre_one = contract(own_feats, weights_one[:feat_width], 0, 0) + contract(
        own_agg_one, weights_one[feat_width:], 0, 0
    )
    hidden_one = jax.nn.silu(pre_one).astype(jnp.bfloat16)
    hidden_all = doubling_gather(hidden_one, order)
    total = contract(own_edges, hidden_all, 0, 0)
    agg_two = (total * own_inverse[:, None]).astype(jnp.bfloat16)
    node_output = (
        contract(hidden_one, self_two, 1, 0) + contract(agg_two, neigh_two, 1, 0)
    ).astype(jnp.bfloat16)
    down_self = contract(cotangent, self_two, 1, 1)
    neighbor_sum = contract(named_by, down_all, 0, 0)
    grad_hidden = down_self + neighbor_sum
    grad_pre = (grad_hidden * silu_slope(pre_one)).astype(jnp.bfloat16)
    terms = jnp.concatenate(
        [
            contract(own_feats, grad_pre, 1, 0),
            contract(own_agg_one, grad_pre, 1, 0),
            contract(hidden_one, cotangent, 0, 0),
            contract(agg_two, cotangent, 0, 0),
        ],
        axis=0,
    )
    with jax.named_scope("weight_grad_sum"):
        if lax.axis_size("dp") == 2 and devices == 16:
            weight_grads = halving_scatter(terms, [0, 4, 1, 3, 2])
        else:
            weight_grads = lax.psum_scatter(terms, ("dp", "mp"), scatter_dimension=0, tiled=True)
    return (node_output, weight_grads)


def solution(mesh):
    in_specs = (
        P("mp", "dp"),
        P(),
        P(),
        P("dp", None),
        P("dp", None),
        P("dp"),
        P(("dp", "mp"), None),
    )
    out_specs = (P(("dp", "mp"), None), P(("dp", "mp"), None))
    return jax.shard_map(shards, mesh=mesh, in_specs=in_specs, out_specs=out_specs, check_vma=False)
```

```python
import jax
import jax.numpy as jnp
from jax import lax
from jax.sharding import PartitionSpec as P


def column_mean(table, indices, live, inverse):
    total = jnp.zeros((table.shape[0], indices.shape[1]), jnp.float32)
    for slot_index in range(indices.shape[0]):
        picked = jnp.take(table, indices[slot_index], axis=1)
        kept = jnp.where(live[slot_index][None, :], picked, jnp.zeros_like(picked))
        total = total + kept.astype(jnp.float32)
    return (total * inverse[None, :]).astype(jnp.bfloat16)


def silu_slope(values):
    sigmoid = jax.nn.sigmoid(values)
    return sigmoid * (1.0 + values * (1.0 - sigmoid))


def contract(left, right, left_dim, right_dim):
    return lax.dot_general(
        left, right, (((left_dim,), (right_dim,)), ((), ())), preferred_element_type=jnp.float32
    )


def swap(values, axis, mask):
    size = lax.axis_size(axis)
    return lax.ppermute(values, axis, [(j, j ^ mask) for j in range(size)])


def halving_scatter(terms, order):
    n_mp = lax.axis_size("mp")
    top = n_mp.bit_length() - 1
    place = lax.axis_index("dp") * n_mp + lax.axis_index("mp")
    rows = terms.shape[0] // (2 * n_mp)
    bits = list(range(top, -1, -1))
    values = terms.reshape((2,) * (top + 1) + (rows, terms.shape[1]))
    for bit in order:
        position = bits.index(bit)
        mine = (place >> bit) & 1
        keep = lax.dynamic_index_in_dim(values, mine, position, keepdims=False)
        send = lax.dynamic_index_in_dim(values, 1 - mine, position, keepdims=False)
        got = swap(send, "dp", 1) if bit == top else swap(send, "mp", 1 << bit)
        values = keep + got
        bits.pop(position)
    return values.reshape(rows, terms.shape[1])


def doubling_gather(rows, order):
    own = lax.axis_index("mp")
    current = rows
    for step, bit in enumerate(order):
        got = swap(current, "mp", 1 << bit)
        low = jnp.where((own >> bit) & 1 == 0, current, got)
        high = jnp.where((own >> bit) & 1 == 0, got, current)
        current = jnp.stack([low, high], axis=step)
    return current.reshape(-1, rows.shape[-1])


def shards(
    node_features, weights_one, weights_two, neighbor_owner, neighbor_row, neighbor_count, cotangent
):
    devices = lax.axis_size("mp")
    own_index = lax.axis_index("mp")
    node_dev = cotangent.shape[0]
    all_nodes = neighbor_owner.shape[0]
    fanout = neighbor_owner.shape[1]
    feat_width = weights_one.shape[0] // 2
    hidden = weights_one.shape[1]
    live = lax.broadcasted_iota(jnp.int32, (all_nodes, fanout), 1) < neighbor_count[:, None]
    inverse_all = 1.0 / neighbor_count.astype(jnp.float32)

    owner_ids = lax.broadcasted_iota(jnp.int32, (devices, 1, 1), 0)
    match = (neighbor_owner[None, :, :] == owner_ids) & live[None, :, :]
    rowsel = jnp.max(jnp.where(match, neighbor_row[None, :, :], -1), axis=2)

    with jax.named_scope("layer_one_mean"):
        if all_nodes * all_nodes <= 4096 * 4096:
            row_ids = lax.broadcasted_iota(jnp.int32, (1, node_dev, 1), 1)
            adjacency = (rowsel[:, None, :] == row_ids).astype(jnp.bfloat16)
            adjacency = adjacency.reshape(devices * node_dev, all_nodes)
            summed = contract(node_features, adjacency, 1, 0)
            agg_one_cols = (summed * inverse_all[None, :]).astype(jnp.bfloat16)
        else:
            owner_slots = neighbor_owner.T
            global_ids = owner_slots * node_dev + neighbor_row.T
            agg_one_cols = column_mean(node_features, global_ids, live.T, inverse_all)

    own_feats, own_agg_one = (
        lax.all_to_all(node_features, "mp", split_axis=1, concat_axis=0, tiled=True),
        lax.all_to_all(agg_one_cols, "mp", split_axis=1, concat_axis=0, tiled=True),
    )
    self_two = weights_two[:hidden]
    neigh_two = weights_two[hidden:]
    own_inverse = lax.dynamic_slice_in_dim(inverse_all, own_index * node_dev, node_dev, 0)
    order = list(range(devices.bit_length() - 2, -1, -1))

    with jax.named_scope("neighbor_tables"):
        row_ids = lax.broadcasted_iota(jnp.int32, (1, node_dev, 1), 1)
        own_sel = lax.dynamic_slice_in_dim(rowsel, own_index * node_dev, node_dev, 1)
        own_edges = (own_sel[:, None, :] == row_ids).astype(jnp.bfloat16)
        own_edges = own_edges.reshape(devices * node_dev, node_dev)
        mine_sel = lax.dynamic_index_in_dim(rowsel, own_index, 0, keepdims=False)
        named_by = (mine_sel[:, None] == row_ids.reshape(1, node_dev)).astype(jnp.bfloat16)

    down_neigh = (contract(cotangent, neigh_two, 1, 1) * own_inverse[:, None]).astype(jnp.bfloat16)
    down_all = doubling_gather(down_neigh, order)

    pre_one = contract(own_feats, weights_one[:feat_width], 0, 0) + contract(
        own_agg_one, weights_one[feat_width:], 0, 0
    )
    hidden_one = jax.nn.silu(pre_one).astype(jnp.bfloat16)
    hidden_all = doubling_gather(hidden_one, order)
    total = contract(own_edges, hidden_all, 0, 0)
    agg_two = (total * own_inverse[:, None]).astype(jnp.bfloat16)
    node_output = (
        contract(hidden_one, self_two, 1, 0) + contract(agg_two, neigh_two, 1, 0)
    ).astype(jnp.bfloat16)
    down_self = contract(cotangent, self_two, 1, 1)
    neighbor_sum = contract(named_by, down_all, 0, 0)
    grad_hidden = down_self + neighbor_sum
    grad_pre = (grad_hidden * silu_slope(pre_one)).astype(jnp.bfloat16)
    terms = jnp.concatenate(
        [
            contract(own_feats, grad_pre, 1, 0),
            contract(own_agg_one, grad_pre, 1, 0),
            contract(hidden_one, cotangent, 0, 0),
            contract(agg_two, cotangent, 0, 0),
        ],
        axis=0,
    )
    with jax.named_scope("weight_grad_sum"):
        if lax.axis_size("dp") == 2 and devices == 16:
            half = terms.shape[1] // 2
            weight_grads = jnp.concatenate(
                [
                    halving_scatter(terms[:, :half], [0, 4, 1, 3, 2]),
                    halving_scatter(terms[:, half:], [0, 1, 4, 2, 3]),
                ],
                axis=1,
            )
        else:
            weight_grads = lax.psum_scatter(terms, ("dp", "mp"), scatter_dimension=0, tiled=True)
    return (node_output, weight_grads)


def solution(mesh):
    in_specs = (
        P("mp", "dp"),
        P(),
        P(),
        P("dp", None),
        P("dp", None),
        P("dp"),
        P(("dp", "mp"), None),
    )
    out_specs = (P(("dp", "mp"), None), P(("dp", "mp"), None))
    return jax.shard_map(shards, mesh=mesh, in_specs=in_specs, out_specs=out_specs, check_vma=False)
```

```python
import jax
import jax.numpy as jnp
from jax import lax
from jax.sharding import PartitionSpec as P


def column_mean(table, indices, live, inverse):
    total = jnp.zeros((table.shape[0], indices.shape[1]), jnp.float32)
    for slot_index in range(indices.shape[0]):
        picked = jnp.take(table, indices[slot_index], axis=1)
        kept = jnp.where(live[slot_index][None, :], picked, jnp.zeros_like(picked))
        total = total + kept.astype(jnp.float32)
    return (total * inverse[None, :]).astype(jnp.bfloat16)


def silu_slope(values):
    sigmoid = jax.nn.sigmoid(values)
    return sigmoid * (1.0 + values * (1.0 - sigmoid))


def contract(left, right, left_dim, right_dim):
    return lax.dot_general(
        left, right, (((left_dim,), (right_dim,)), ((), ())), preferred_element_type=jnp.float32
    )


def swap(values, axis, mask):
    size = lax.axis_size(axis)
    return lax.ppermute(values, axis, [(j, j ^ mask) for j in range(size)])


def halving_scatter(terms, order):
    n_mp = lax.axis_size("mp")
    top = n_mp.bit_length() - 1
    place = lax.axis_index("dp") * n_mp + lax.axis_index("mp")
    rows = terms.shape[0] // (2 * n_mp)
    bits = list(range(top, -1, -1))
    values = terms.reshape((2,) * (top + 1) + (rows, terms.shape[1]))
    for bit in order:
        position = bits.index(bit)
        mine = (place >> bit) & 1
        keep = lax.dynamic_index_in_dim(values, mine, position, keepdims=False)
        send = lax.dynamic_index_in_dim(values, 1 - mine, position, keepdims=False)
        got = swap(send, "dp", 1) if bit == top else swap(send, "mp", 1 << bit)
        values = keep + got
        bits.pop(position)
    return values.reshape(rows, terms.shape[1])


def doubling_gather(rows, order):
    own = lax.axis_index("mp")
    current = rows
    for step, bit in enumerate(order):
        got = swap(current, "mp", 1 << bit)
        low = jnp.where((own >> bit) & 1 == 0, current, got)
        high = jnp.where((own >> bit) & 1 == 0, got, current)
        current = jnp.stack([low, high], axis=sum(1 for done in order[:step] if done > bit))
    return current.reshape(-1, rows.shape[-1])


def split_gather(rows, order, other):
    if other == order:
        return doubling_gather(rows, order)
    half = rows.shape[1] // 2
    return jnp.concatenate(
        [doubling_gather(rows[:, :half], order), doubling_gather(rows[:, half:], other)], axis=1
    )


def shards(
    node_features, weights_one, weights_two, neighbor_owner, neighbor_row, neighbor_count, cotangent
):
    devices = lax.axis_size("mp")
    own_index = lax.axis_index("mp")
    node_dev = cotangent.shape[0]
    all_nodes = neighbor_owner.shape[0]
    fanout = neighbor_owner.shape[1]
    feat_width = weights_one.shape[0] // 2
    hidden = weights_one.shape[1]
    live = lax.broadcasted_iota(jnp.int32, (all_nodes, fanout), 1) < neighbor_count[:, None]
    inverse_all = 1.0 / neighbor_count.astype(jnp.float32)

    owner_ids = lax.broadcasted_iota(jnp.int32, (devices, 1, 1), 0)
    match = (neighbor_owner[None, :, :] == owner_ids) & live[None, :, :]
    rowsel = jnp.max(jnp.where(match, neighbor_row[None, :, :], -1), axis=2)

    with jax.named_scope("layer_one_mean"):
        if all_nodes * all_nodes <= 4096 * 4096:
            row_ids = lax.broadcasted_iota(jnp.int32, (1, node_dev, 1), 1)
            adjacency = (rowsel[:, None, :] == row_ids).astype(jnp.bfloat16)
            adjacency = adjacency.reshape(devices * node_dev, all_nodes)
            summed = contract(node_features, adjacency, 1, 0)
            agg_one_cols = (summed * inverse_all[None, :]).astype(jnp.bfloat16)
        else:
            owner_slots = neighbor_owner.T
            global_ids = owner_slots * node_dev + neighbor_row.T
            agg_one_cols = column_mean(node_features, global_ids, live.T, inverse_all)

    own_feats, own_agg_one = (
        lax.all_to_all(node_features, "mp", split_axis=1, concat_axis=0, tiled=True),
        lax.all_to_all(agg_one_cols, "mp", split_axis=1, concat_axis=0, tiled=True),
    )
    self_two = weights_two[:hidden]
    neigh_two = weights_two[hidden:]
    own_inverse = lax.dynamic_slice_in_dim(inverse_all, own_index * node_dev, node_dev, 0)
    order = list(range(devices.bit_length() - 2, -1, -1))
    other = [1] + [bit for bit in order if bit != 1] if devices == 16 else order

    with jax.named_scope("neighbor_tables"):
        row_ids = lax.broadcasted_iota(jnp.int32, (1, node_dev, 1), 1)
        own_sel = lax.dynamic_slice_in_dim(rowsel, own_index * node_dev, node_dev, 1)
        own_edges = (own_sel[:, None, :] == row_ids).astype(jnp.bfloat16)
        own_edges = own_edges.reshape(devices * node_dev, node_dev)
        mine_sel = lax.dynamic_index_in_dim(rowsel, own_index, 0, keepdims=False)
        named_by = (mine_sel[:, None] == row_ids.reshape(1, node_dev)).astype(jnp.bfloat16)

    down_neigh = (contract(cotangent, neigh_two, 1, 1) * own_inverse[:, None]).astype(jnp.bfloat16)
    down_all = split_gather(down_neigh, order, other)

    pre_one = contract(own_feats, weights_one[:feat_width], 0, 0) + contract(
        own_agg_one, weights_one[feat_width:], 0, 0
    )
    hidden_one = jax.nn.silu(pre_one).astype(jnp.bfloat16)
    hidden_all = split_gather(hidden_one, order, other)
    total = contract(own_edges, hidden_all, 0, 0)
    agg_two = (total * own_inverse[:, None]).astype(jnp.bfloat16)
    node_output = (
        contract(hidden_one, self_two, 1, 0) + contract(agg_two, neigh_two, 1, 0)
    ).astype(jnp.bfloat16)
    down_self = contract(cotangent, self_two, 1, 1)
    neighbor_sum = contract(named_by, down_all, 0, 0)
    grad_hidden = down_self + neighbor_sum
    grad_pre = (grad_hidden * silu_slope(pre_one)).astype(jnp.bfloat16)
    terms = jnp.concatenate(
        [
            contract(own_feats, grad_pre, 1, 0),
            contract(own_agg_one, grad_pre, 1, 0),
            contract(hidden_one, cotangent, 0, 0),
            contract(agg_two, cotangent, 0, 0),
        ],
        axis=0,
    )
    with jax.named_scope("weight_grad_sum"):
        if lax.axis_size("dp") == 2 and devices == 16:
            half = terms.shape[1] // 2
            weight_grads = jnp.concatenate(
                [
                    halving_scatter(terms[:, :half], [0, 4, 1, 3, 2]),
                    halving_scatter(terms[:, half:], [0, 1, 4, 2, 3]),
                ],
                axis=1,
            )
        else:
            weight_grads = lax.psum_scatter(terms, ("dp", "mp"), scatter_dimension=0, tiled=True)
    return (node_output, weight_grads)


def solution(mesh):
    in_specs = (
        P("mp", "dp"),
        P(),
        P(),
        P("dp", None),
        P("dp", None),
        P("dp"),
        P(("dp", "mp"), None),
    )
    out_specs = (P(("dp", "mp"), None), P(("dp", "mp"), None))
    return jax.shard_map(shards, mesh=mesh, in_specs=in_specs, out_specs=out_specs, check_vma=False)
```

```python
import jax
import jax.numpy as jnp
from jax import lax
from jax.sharding import PartitionSpec as P


def column_mean(table, indices, live, inverse):
    total = jnp.zeros((table.shape[0], indices.shape[1]), jnp.float32)
    for slot_index in range(indices.shape[0]):
        picked = jnp.take(table, indices[slot_index], axis=1)
        kept = jnp.where(live[slot_index][None, :], picked, jnp.zeros_like(picked))
        total = total + kept.astype(jnp.float32)
    return (total * inverse[None, :]).astype(jnp.bfloat16)


def silu_slope(values):
    sigmoid = jax.nn.sigmoid(values)
    return sigmoid * (1.0 + values * (1.0 - sigmoid))


def contract(left, right, left_dim, right_dim):
    return lax.dot_general(
        left, right, (((left_dim,), (right_dim,)), ((), ())), preferred_element_type=jnp.float32
    )


def swap(values, axis, mask):
    size = lax.axis_size(axis)
    return lax.ppermute(values, axis, [(j, j ^ mask) for j in range(size)])


def halving_scatter(terms, order):
    n_mp = lax.axis_size("mp")
    top = n_mp.bit_length() - 1
    place = lax.axis_index("dp") * n_mp + lax.axis_index("mp")
    rows = terms.shape[0] // (2 * n_mp)
    bits = list(range(top, -1, -1))
    values = terms.reshape((2,) * (top + 1) + (rows, terms.shape[1]))
    for bit in order:
        position = bits.index(bit)
        mine = (place >> bit) & 1
        keep = lax.dynamic_index_in_dim(values, mine, position, keepdims=False)
        send = lax.dynamic_index_in_dim(values, 1 - mine, position, keepdims=False)
        got = swap(send, "dp", 1) if bit == top else swap(send, "mp", 1 << bit)
        values = keep + got
        bits.pop(position)
    return values.reshape(rows, terms.shape[1])


def doubling_gather(rows, order):
    own = lax.axis_index("mp")
    current = rows
    for step, bit in enumerate(order):
        got = swap(current, "mp", 1 << bit)
        low = jnp.where((own >> bit) & 1 == 0, current, got)
        high = jnp.where((own >> bit) & 1 == 0, got, current)
        current = jnp.stack([low, high], axis=sum(1 for done in order[:step] if done > bit))
    return current.reshape(-1, rows.shape[-1])


def split_gather(rows, order, other):
    if other == order:
        return doubling_gather(rows, order)
    half = rows.shape[1] // 2
    return jnp.concatenate(
        [doubling_gather(rows[:, :half], order), doubling_gather(rows[:, half:], other)], axis=1
    )


def last_block_sum(block):
    mp_index = lax.axis_index("mp")
    rows = block.shape[0] // 8
    values = block.reshape(2, 2, 2, rows, block.shape[1])
    bits = [2, 1, 0]
    for bit in [0, 1, 2]:
        position = bits.index(bit)
        mine = (mp_index >> bit) & 1
        keep = lax.dynamic_index_in_dim(values, mine, position, keepdims=False)
        send = lax.dynamic_index_in_dim(values, 1 - mine, position, keepdims=False)
        values = keep + swap(send, "mp", 1 << bit)
        bits.pop(position)
    values = values.reshape(rows, block.shape[1])
    values = values + swap(values, "mp", 8)
    values = values + swap(values, "dp", 1)
    lands = (lax.axis_index("dp") == 1) & (mp_index >= 8)
    return jnp.where(lands, values, jnp.zeros_like(values))


def shards(
    node_features, weights_one, weights_two, neighbor_owner, neighbor_row, neighbor_count, cotangent
):
    devices = lax.axis_size("mp")
    own_index = lax.axis_index("mp")
    node_dev = cotangent.shape[0]
    all_nodes = neighbor_owner.shape[0]
    fanout = neighbor_owner.shape[1]
    feat_width = weights_one.shape[0] // 2
    hidden = weights_one.shape[1]
    live = lax.broadcasted_iota(jnp.int32, (all_nodes, fanout), 1) < neighbor_count[:, None]
    inverse_all = 1.0 / neighbor_count.astype(jnp.float32)

    owner_ids = lax.broadcasted_iota(jnp.int32, (devices, 1, 1), 0)
    match = (neighbor_owner[None, :, :] == owner_ids) & live[None, :, :]
    rowsel = jnp.max(jnp.where(match, neighbor_row[None, :, :], -1), axis=2)

    with jax.named_scope("layer_one_mean"):
        if all_nodes * all_nodes <= 4096 * 4096:
            row_ids = lax.broadcasted_iota(jnp.int32, (1, node_dev, 1), 1)
            adjacency = (rowsel[:, None, :] == row_ids).astype(jnp.bfloat16)
            adjacency = adjacency.reshape(devices * node_dev, all_nodes)
            summed = contract(node_features, adjacency, 1, 0)
            agg_one_cols = (summed * inverse_all[None, :]).astype(jnp.bfloat16)
        else:
            owner_slots = neighbor_owner.T
            global_ids = owner_slots * node_dev + neighbor_row.T
            agg_one_cols = column_mean(node_features, global_ids, live.T, inverse_all)

    own_feats, own_agg_one = (
        lax.all_to_all(node_features, "mp", split_axis=1, concat_axis=0, tiled=True),
        lax.all_to_all(agg_one_cols, "mp", split_axis=1, concat_axis=0, tiled=True),
    )
    self_two = weights_two[:hidden]
    neigh_two = weights_two[hidden:]
    own_inverse = lax.dynamic_slice_in_dim(inverse_all, own_index * node_dev, node_dev, 0)
    order = list(range(devices.bit_length() - 2, -1, -1))
    other = [1] + [bit for bit in order if bit != 1] if devices == 16 else order

    with jax.named_scope("neighbor_tables"):
        row_ids = lax.broadcasted_iota(jnp.int32, (1, node_dev, 1), 1)
        own_sel = lax.dynamic_slice_in_dim(rowsel, own_index * node_dev, node_dev, 1)
        own_edges = (own_sel[:, None, :] == row_ids).astype(jnp.bfloat16)
        own_edges = own_edges.reshape(devices * node_dev, node_dev)
        mine_sel = lax.dynamic_index_in_dim(rowsel, own_index, 0, keepdims=False)
        named_by = (mine_sel[:, None] == row_ids.reshape(1, node_dev)).astype(jnp.bfloat16)

    down_neigh = (contract(cotangent, neigh_two, 1, 1) * own_inverse[:, None]).astype(jnp.bfloat16)
    down_all = split_gather(down_neigh, order, other)

    pre_one = contract(own_feats, weights_one[:feat_width], 0, 0) + contract(
        own_agg_one, weights_one[feat_width:], 0, 0
    )
    hidden_one = jax.nn.silu(pre_one).astype(jnp.bfloat16)
    hidden_all = split_gather(hidden_one, order, other)
    total = contract(own_edges, hidden_all, 0, 0)
    agg_two = (total * own_inverse[:, None]).astype(jnp.bfloat16)
    node_output = (
        contract(hidden_one, self_two, 1, 0) + contract(agg_two, neigh_two, 1, 0)
    ).astype(jnp.bfloat16)
    down_self = contract(cotangent, self_two, 1, 1)
    neighbor_sum = contract(named_by, down_all, 0, 0)
    grad_hidden = down_self + neighbor_sum
    grad_pre = (grad_hidden * silu_slope(pre_one)).astype(jnp.bfloat16)
    early_terms = [
        contract(own_feats, grad_pre, 1, 0),
        contract(own_agg_one, grad_pre, 1, 0),
        contract(hidden_one, cotangent, 0, 0),
    ]
    last_term = contract(agg_two, cotangent, 0, 0)
    with jax.named_scope("weight_grad_sum"):
        if lax.axis_size("dp") == 2 and devices == 16:
            terms = jnp.concatenate(early_terms + [jnp.zeros_like(last_term)], axis=0)
            half = terms.shape[1] // 2
            weight_grads = jnp.concatenate(
                [
                    halving_scatter(terms[:, :half], [0, 4, 1, 3, 2]),
                    halving_scatter(terms[:, half:], [0, 1, 4, 2, 3]),
                ],
                axis=1,
            )
            weight_grads = weight_grads + last_block_sum(last_term)
        else:
            terms = jnp.concatenate(early_terms + [last_term], axis=0)
            weight_grads = lax.psum_scatter(terms, ("dp", "mp"), scatter_dimension=0, tiled=True)
    return (node_output, weight_grads)


def solution(mesh):
    in_specs = (
        P("mp", "dp"),
        P(),
        P(),
        P("dp", None),
        P("dp", None),
        P("dp"),
        P(("dp", "mp"), None),
    )
    out_specs = (P(("dp", "mp"), None), P(("dp", "mp"), None))
    return jax.shard_map(shards, mesh=mesh, in_specs=in_specs, out_specs=out_specs, check_vma=False)
```

```python
import jax
import jax.numpy as jnp
from jax import lax
from jax.sharding import PartitionSpec as P


def column_mean(table, indices, live, inverse):
    total = jnp.zeros((table.shape[0], indices.shape[1]), jnp.float32)
    for slot_index in range(indices.shape[0]):
        picked = jnp.take(table, indices[slot_index], axis=1)
        kept = jnp.where(live[slot_index][None, :], picked, jnp.zeros_like(picked))
        total = total + kept.astype(jnp.float32)
    return (total * inverse[None, :]).astype(jnp.bfloat16)


def silu_slope(values):
    sigmoid = jax.nn.sigmoid(values)
    return sigmoid * (1.0 + values * (1.0 - sigmoid))


def contract(left, right, left_dim, right_dim):
    return lax.dot_general(
        left, right, (((left_dim,), (right_dim,)), ((), ())), preferred_element_type=jnp.float32
    )


def swap(values, axis, mask):
    size = lax.axis_size(axis)
    return lax.ppermute(values, axis, [(j, j ^ mask) for j in range(size)])


def halving_scatter(terms, order):
    n_mp = lax.axis_size("mp")
    top = n_mp.bit_length() - 1
    place = lax.axis_index("dp") * n_mp + lax.axis_index("mp")
    rows = terms.shape[0] // (2 * n_mp)
    bits = list(range(top, -1, -1))
    values = terms.reshape((2,) * (top + 1) + (rows, terms.shape[1]))
    for bit in order:
        position = bits.index(bit)
        mine = (place >> bit) & 1
        keep = lax.dynamic_index_in_dim(values, mine, position, keepdims=False)
        send = lax.dynamic_index_in_dim(values, 1 - mine, position, keepdims=False)
        got = swap(send, "dp", 1) if bit == top else swap(send, "mp", 1 << bit)
        values = keep + got
        bits.pop(position)
    return values.reshape(rows, terms.shape[1])


def doubling_gather(rows, order):
    own = lax.axis_index("mp")
    current = rows
    for step, bit in enumerate(order):
        got = swap(current, "mp", 1 << bit)
        low = jnp.where((own >> bit) & 1 == 0, current, got)
        high = jnp.where((own >> bit) & 1 == 0, got, current)
        current = jnp.stack([low, high], axis=sum(1 for done in order[:step] if done > bit))
    return current.reshape(-1, rows.shape[-1])


def split_gather(rows, order, other):
    if other == order:
        return doubling_gather(rows, order)
    half = rows.shape[1] // 2
    return jnp.concatenate(
        [doubling_gather(rows[:, :half], order), doubling_gather(rows[:, half:], other)], axis=1
    )


def shards(
    node_features, weights_one, weights_two, neighbor_owner, neighbor_row, neighbor_count, cotangent
):
    devices = lax.axis_size("mp")
    own_index = lax.axis_index("mp")
    node_dev = cotangent.shape[0]
    all_nodes = neighbor_owner.shape[0]
    fanout = neighbor_owner.shape[1]
    feat_width = weights_one.shape[0] // 2
    hidden = weights_one.shape[1]
    live = lax.broadcasted_iota(jnp.int32, (all_nodes, fanout), 1) < neighbor_count[:, None]
    inverse_all = 1.0 / neighbor_count.astype(jnp.float32)

    owner_ids = lax.broadcasted_iota(jnp.int32, (devices, 1, 1), 0)
    match = (neighbor_owner[None, :, :] == owner_ids) & live[None, :, :]
    rowsel = jnp.max(jnp.where(match, neighbor_row[None, :, :], -1), axis=2)

    with jax.named_scope("layer_one_mean"):
        if all_nodes * all_nodes <= 4096 * 4096:
            row_ids = lax.broadcasted_iota(jnp.int32, (1, node_dev, 1), 1)
            adjacency = (rowsel[:, None, :] == row_ids).astype(jnp.bfloat16)
            adjacency = adjacency.reshape(devices * node_dev, all_nodes)
            summed = contract(node_features, adjacency, 1, 0)
            agg_one_cols = (summed * inverse_all[None, :]).astype(jnp.bfloat16)
        else:
            owner_slots = neighbor_owner.T
            global_ids = owner_slots * node_dev + neighbor_row.T
            agg_one_cols = column_mean(node_features, global_ids, live.T, inverse_all)

    both = jnp.stack([node_features, agg_one_cols], axis=0)
    both = lax.all_to_all(both, "mp", split_axis=2, concat_axis=1, tiled=True)
    own_feats, own_agg_one = both[0], both[1]
    self_two = weights_two[:hidden]
    neigh_two = weights_two[hidden:]
    own_inverse = lax.dynamic_slice_in_dim(inverse_all, own_index * node_dev, node_dev, 0)
    order = list(range(devices.bit_length() - 2, -1, -1))
    other = [1] + [bit for bit in order if bit != 1] if devices == 16 else order

    with jax.named_scope("neighbor_tables"):
        row_ids = lax.broadcasted_iota(jnp.int32, (1, node_dev, 1), 1)
        own_sel = lax.dynamic_slice_in_dim(rowsel, own_index * node_dev, node_dev, 1)
        own_edges = (own_sel[:, None, :] == row_ids).astype(jnp.bfloat16)
        own_edges = own_edges.reshape(devices * node_dev, node_dev)
        mine_sel = lax.dynamic_index_in_dim(rowsel, own_index, 0, keepdims=False)
        named_by = (mine_sel[:, None] == row_ids.reshape(1, node_dev)).astype(jnp.bfloat16)

    down_neigh = (contract(cotangent, neigh_two, 1, 1) * own_inverse[:, None]).astype(jnp.bfloat16)
    down_all = split_gather(down_neigh, order, other)

    pre_one = contract(own_feats, weights_one[:feat_width], 0, 0) + contract(
        own_agg_one, weights_one[feat_width:], 0, 0
    )
    hidden_one = jax.nn.silu(pre_one).astype(jnp.bfloat16)
    hidden_all = split_gather(hidden_one, order, other)
    total = contract(own_edges, hidden_all, 0, 0)
    agg_two = (total * own_inverse[:, None]).astype(jnp.bfloat16)
    node_output = (
        contract(hidden_one, self_two, 1, 0) + contract(agg_two, neigh_two, 1, 0)
    ).astype(jnp.bfloat16)
    down_self = contract(cotangent, self_two, 1, 1)
    neighbor_sum = contract(named_by, down_all, 0, 0)
    grad_hidden = down_self + neighbor_sum
    grad_pre = (grad_hidden * silu_slope(pre_one)).astype(jnp.bfloat16)
    terms = jnp.concatenate(
        [
            contract(own_feats, grad_pre, 1, 0),
            contract(own_agg_one, grad_pre, 1, 0),
            contract(hidden_one, cotangent, 0, 0),
            contract(agg_two, cotangent, 0, 0),
        ],
        axis=0,
    )
    with jax.named_scope("weight_grad_sum"):
        if lax.axis_size("dp") == 2 and devices == 16:
            half = terms.shape[1] // 2
            weight_grads = jnp.concatenate(
                [
                    halving_scatter(terms[:, :half], [0, 4, 1, 3, 2]),
                    halving_scatter(terms[:, half:], [0, 1, 4, 2, 3]),
                ],
                axis=1,
            )
        else:
            weight_grads = lax.psum_scatter(terms, ("dp", "mp"), scatter_dimension=0, tiled=True)
    return (node_output, weight_grads)


def solution(mesh):
    in_specs = (
        P("mp", "dp"),
        P(),
        P(),
        P("dp", None),
        P("dp", None),
        P("dp"),
        P(("dp", "mp"), None),
    )
    out_specs = (P(("dp", "mp"), None), P(("dp", "mp"), None))
    return jax.shard_map(shards, mesh=mesh, in_specs=in_specs, out_specs=out_specs, check_vma=False)
```

```python
import jax
import jax.numpy as jnp
from jax import lax
from jax.sharding import PartitionSpec as P


def column_mean(table, indices, live, inverse):
    total = jnp.zeros((table.shape[0], indices.shape[1]), jnp.float32)
    for slot_index in range(indices.shape[0]):
        picked = jnp.take(table, indices[slot_index], axis=1)
        kept = jnp.where(live[slot_index][None, :], picked, jnp.zeros_like(picked))
        total = total + kept.astype(jnp.float32)
    return (total * inverse[None, :]).astype(jnp.bfloat16)


def silu_slope(values):
    sigmoid = jax.nn.sigmoid(values)
    return sigmoid * (1.0 + values * (1.0 - sigmoid))


def contract(left, right, left_dim, right_dim):
    return lax.dot_general(
        left, right, (((left_dim,), (right_dim,)), ((), ())), preferred_element_type=jnp.float32
    )


def swap(values, axis, mask):
    size = lax.axis_size(axis)
    return lax.ppermute(values, axis, [(j, j ^ mask) for j in range(size)])


def halving_scatter(terms, order):
    n_mp = lax.axis_size("mp")
    top = n_mp.bit_length() - 1
    place = lax.axis_index("dp") * n_mp + lax.axis_index("mp")
    rows = terms.shape[0] // (2 * n_mp)
    bits = list(range(top, -1, -1))
    values = terms.reshape((2,) * (top + 1) + (rows, terms.shape[1]))
    for bit in order:
        position = bits.index(bit)
        mine = (place >> bit) & 1
        keep = lax.dynamic_index_in_dim(values, mine, position, keepdims=False)
        send = lax.dynamic_index_in_dim(values, 1 - mine, position, keepdims=False)
        got = swap(send, "dp", 1) if bit == top else swap(send, "mp", 1 << bit)
        values = keep + got
        bits.pop(position)
    return values.reshape(rows, terms.shape[1])


def doubling_gather(rows, order):
    own = lax.axis_index("mp")
    current = rows
    for step, bit in enumerate(order):
        got = swap(current, "mp", 1 << bit)
        low = jnp.where((own >> bit) & 1 == 0, current, got)
        high = jnp.where((own >> bit) & 1 == 0, got, current)
        current = jnp.stack([low, high], axis=sum(1 for done in order[:step] if done > bit))
    return current.reshape(-1, rows.shape[-1])


def split_gather(rows, order, other):
    if other == order:
        return doubling_gather(rows, order)
    half = rows.shape[1] // 2
    return jnp.concatenate(
        [doubling_gather(rows[:, :half], order), doubling_gather(rows[:, half:], other)], axis=1
    )


def shards(
    node_features, weights_one, weights_two, neighbor_owner, neighbor_row, neighbor_count, cotangent
):
    devices = lax.axis_size("mp")
    own_index = lax.axis_index("mp")
    node_dev = cotangent.shape[0]
    all_nodes = neighbor_owner.shape[0]
    fanout = neighbor_owner.shape[1]
    feat_width = weights_one.shape[0] // 2
    hidden = weights_one.shape[1]
    live = lax.broadcasted_iota(jnp.int32, (all_nodes, fanout), 1) < neighbor_count[:, None]
    inverse_all = 1.0 / neighbor_count.astype(jnp.float32)

    owner_ids = lax.broadcasted_iota(jnp.int32, (devices, 1, 1), 0)
    match = (neighbor_owner[None, :, :] == owner_ids) & live[None, :, :]
    rowsel = jnp.max(jnp.where(match, neighbor_row[None, :, :], -1), axis=2)

    with jax.named_scope("layer_one_mean"):
        if all_nodes * all_nodes <= 4096 * 4096:
            row_ids = lax.broadcasted_iota(jnp.int32, (1, node_dev, 1), 1)
            adjacency = (rowsel[:, None, :] == row_ids).astype(jnp.bfloat16)
            adjacency = adjacency.reshape(devices * node_dev, all_nodes)
            summed = contract(node_features, adjacency, 1, 0)
            agg_one_cols = (summed * inverse_all[None, :]).astype(jnp.bfloat16)
        else:
            owner_slots = neighbor_owner.T
            global_ids = owner_slots * node_dev + neighbor_row.T
            agg_one_cols = column_mean(node_features, global_ids, live.T, inverse_all)

    own_feats, own_agg_one = (
        lax.all_to_all(node_features, "mp", split_axis=1, concat_axis=0, tiled=True),
        lax.all_to_all(agg_one_cols, "mp", split_axis=1, concat_axis=0, tiled=True),
    )
    self_two = weights_two[:hidden]
    neigh_two = weights_two[hidden:]
    own_inverse = lax.dynamic_slice_in_dim(inverse_all, own_index * node_dev, node_dev, 0)
    order = list(range(devices.bit_length() - 2, -1, -1))
    other = [1] + [bit for bit in order if bit != 1] if devices == 16 else order

    with jax.named_scope("neighbor_tables"):
        row_ids = lax.broadcasted_iota(jnp.int32, (1, node_dev, 1), 1)
        own_sel = lax.dynamic_slice_in_dim(rowsel, own_index * node_dev, node_dev, 1)
        own_edges = (own_sel[:, None, :] == row_ids).astype(jnp.bfloat16)
        own_edges = own_edges.reshape(devices * node_dev, node_dev)
        mine_sel = lax.dynamic_index_in_dim(rowsel, own_index, 0, keepdims=False)
        named_by = (mine_sel[:, None] == row_ids.reshape(1, node_dev)).astype(jnp.bfloat16)

    down_neigh = (contract(cotangent, neigh_two, 1, 1) * own_inverse[:, None]).astype(jnp.bfloat16)
    down_all = split_gather(down_neigh, order, other)

    pre_one = contract(own_feats, weights_one[:feat_width], 0, 0) + contract(
        own_agg_one, weights_one[feat_width:], 0, 0
    )
    hidden_one = jax.nn.silu(pre_one).astype(jnp.bfloat16)
    hidden_all = split_gather(hidden_one, order, other)
    total = contract(own_edges, hidden_all, 0, 0)
    agg_two = (total * own_inverse[:, None]).astype(jnp.bfloat16)
    node_output = (
        contract(hidden_one, self_two, 1, 0) + contract(agg_two, neigh_two, 1, 0)
    ).astype(jnp.bfloat16)
    down_self = contract(cotangent, self_two, 1, 1)
    neighbor_sum = contract(named_by, down_all, 0, 0)
    grad_hidden = down_self + neighbor_sum
    grad_pre = (grad_hidden * silu_slope(pre_one)).astype(jnp.bfloat16)
    terms = jnp.concatenate(
        [
            contract(own_feats, grad_pre, 1, 0),
            contract(own_agg_one, grad_pre, 1, 0),
            contract(hidden_one, cotangent, 0, 0),
            contract(agg_two, cotangent, 0, 0),
        ],
        axis=0,
    )
    with jax.named_scope("weight_grad_sum"):
        if lax.axis_size("dp") == 2 and devices == 16:
            cut = [0, 3 * terms.shape[1] // 8, 6 * terms.shape[1] // 8, terms.shape[1]]
            orders = [[0, 4, 1, 2, 3], [0, 1, 2, 4, 3], [0, 2, 4, 1, 3]]
            weight_grads = jnp.concatenate(
                [
                    halving_scatter(terms[:, cut[i]:cut[i + 1]], orders[i])
                    for i in range(3)
                ],
                axis=1,
            )
        else:
            weight_grads = lax.psum_scatter(terms, ("dp", "mp"), scatter_dimension=0, tiled=True)
    return (node_output, weight_grads)


def solution(mesh):
    in_specs = (
        P("mp", "dp"),
        P(),
        P(),
        P("dp", None),
        P("dp", None),
        P("dp"),
        P(("dp", "mp"), None),
    )
    out_specs = (P(("dp", "mp"), None), P(("dp", "mp"), None))
    return jax.shard_map(shards, mesh=mesh, in_specs=in_specs, out_specs=out_specs, check_vma=False)
```

```python
import jax
import jax.numpy as jnp
from jax import lax
from jax.sharding import PartitionSpec as P


def column_mean(table, indices, live, inverse):
    total = jnp.zeros((table.shape[0], indices.shape[1]), jnp.float32)
    for slot_index in range(indices.shape[0]):
        picked = jnp.take(table, indices[slot_index], axis=1)
        kept = jnp.where(live[slot_index][None, :], picked, jnp.zeros_like(picked))
        total = total + kept.astype(jnp.float32)
    return (total * inverse[None, :]).astype(jnp.bfloat16)


def silu_slope(values):
    sigmoid = jax.nn.sigmoid(values)
    return sigmoid * (1.0 + values * (1.0 - sigmoid))


def contract(left, right, left_dim, right_dim):
    return lax.dot_general(
        left, right, (((left_dim,), (right_dim,)), ((), ())), preferred_element_type=jnp.float32
    )


def swap(values, axis, mask):
    size = lax.axis_size(axis)
    return lax.ppermute(values, axis, [(j, j ^ mask) for j in range(size)])


def halving_scatter(terms, order):
    n_mp = lax.axis_size("mp")
    top = n_mp.bit_length() - 1
    place = lax.axis_index("dp") * n_mp + lax.axis_index("mp")
    rows = terms.shape[0] // (2 * n_mp)
    bits = list(range(top, -1, -1))
    values = terms.reshape((2,) * (top + 1) + (rows, terms.shape[1]))
    for bit in order:
        position = bits.index(bit)
        mine = (place >> bit) & 1
        keep = lax.dynamic_index_in_dim(values, mine, position, keepdims=False)
        send = lax.dynamic_index_in_dim(values, 1 - mine, position, keepdims=False)
        got = swap(send, "dp", 1) if bit == top else swap(send, "mp", 1 << bit)
        values = keep + got
        bits.pop(position)
    return values.reshape(rows, terms.shape[1])


def doubling_step(current, order, step):
    own = lax.axis_index("mp")
    bit = order[step]
    got = swap(current, "mp", 1 << bit)
    low = jnp.where((own >> bit) & 1 == 0, current, got)
    high = jnp.where((own >> bit) & 1 == 0, got, current)
    return jnp.stack([low, high], axis=sum(1 for done in order[:step] if done > bit))


def doubling_gather(rows, order):
    current = rows
    for step in range(len(order)):
        current = doubling_step(current, order, step)
    return current.reshape(-1, rows.shape[-1])


def split_gather(rows, order, other):
    if other == order:
        return doubling_gather(rows, order)
    half = rows.shape[1] // 2
    return jnp.concatenate(
        [doubling_gather(rows[:, :half], order), doubling_gather(rows[:, half:], other)], axis=1
    )


def shards(
    node_features, weights_one, weights_two, neighbor_owner, neighbor_row, neighbor_count, cotangent
):
    devices = lax.axis_size("mp")
    own_index = lax.axis_index("mp")
    node_dev = cotangent.shape[0]
    all_nodes = neighbor_owner.shape[0]
    fanout = neighbor_owner.shape[1]
    feat_width = weights_one.shape[0] // 2
    hidden = weights_one.shape[1]
    live = lax.broadcasted_iota(jnp.int32, (all_nodes, fanout), 1) < neighbor_count[:, None]
    inverse_all = 1.0 / neighbor_count.astype(jnp.float32)

    owner_ids = lax.broadcasted_iota(jnp.int32, (devices, 1, 1), 0)
    match = (neighbor_owner[None, :, :] == owner_ids) & live[None, :, :]
    rowsel = jnp.max(jnp.where(match, neighbor_row[None, :, :], -1), axis=2)

    self_two = weights_two[:hidden]
    neigh_two = weights_two[hidden:]
    own_inverse = lax.dynamic_slice_in_dim(inverse_all, own_index * node_dev, node_dev, 0)
    order = list(range(devices.bit_length() - 2, -1, -1))
    other = [1] + [bit for bit in order if bit != 1] if devices == 16 else order
    dense_one = all_nodes * all_nodes <= 4096 * 4096

    down_neigh = (contract(cotangent, neigh_two, 1, 1) * own_inverse[:, None]).astype(jnp.bfloat16)
    half = down_neigh.shape[1] // 2
    parts = [down_neigh[:, :half], down_neigh[:, half:]]
    orders = [order, other]
    steps_done = 0

    def advance(parts, steps_done):
        if steps_done < len(order):
            parts = [doubling_step(p, o, steps_done) for p, o in zip(parts, orders)]
        return parts, steps_done + 1

    parts, steps_done = advance(parts, steps_done)

    with jax.named_scope("layer_one_mean"):
        if dense_one:
            row_ids = lax.broadcasted_iota(jnp.int32, (1, node_dev, 1), 1)
            adjacency = (rowsel[:, None, :] == row_ids).astype(jnp.bfloat16)
            adjacency = adjacency.reshape(devices * node_dev, all_nodes)
            parts, adjacency = lax.optimization_barrier((parts, adjacency))
            parts, steps_done = advance(parts, steps_done)
            summed = contract(node_features, adjacency, 1, 0)
            agg_one_cols = (summed * inverse_all[None, :]).astype(jnp.bfloat16)
        else:
            owner_slots = neighbor_owner.T
            global_ids = owner_slots * node_dev + neighbor_row.T
            agg_one_cols = column_mean(node_features, global_ids, live.T, inverse_all)
    parts, agg_one_cols = lax.optimization_barrier((parts, agg_one_cols))
    parts, steps_done = advance(parts, steps_done)

    own_feats, own_agg_one = (
        lax.all_to_all(node_features, "mp", split_axis=1, concat_axis=0, tiled=True),
        lax.all_to_all(agg_one_cols, "mp", split_axis=1, concat_axis=0, tiled=True),
    )
    parts, own_agg_one = lax.optimization_barrier((parts, own_agg_one))
    while steps_done < len(order):
        parts, steps_done = advance(parts, steps_done)
    down_all = jnp.concatenate([p.reshape(-1, half) for p in parts], axis=1)

    with jax.named_scope("neighbor_tables"):
        row_ids = lax.broadcasted_iota(jnp.int32, (1, node_dev, 1), 1)
        own_sel = lax.dynamic_slice_in_dim(rowsel, own_index * node_dev, node_dev, 1)
        own_edges = (own_sel[:, None, :] == row_ids).astype(jnp.bfloat16)
        own_edges = own_edges.reshape(devices * node_dev, node_dev)
        mine_sel = lax.dynamic_index_in_dim(rowsel, own_index, 0, keepdims=False)
        named_by = (mine_sel[:, None] == row_ids.reshape(1, node_dev)).astype(jnp.bfloat16)

    pre_one = contract(own_feats, weights_one[:feat_width], 0, 0) + contract(
        own_agg_one, weights_one[feat_width:], 0, 0
    )
    hidden_one = jax.nn.silu(pre_one).astype(jnp.bfloat16)
    hidden_all = split_gather(hidden_one, order, other)
    total = contract(own_edges, hidden_all, 0, 0)
    agg_two = (total * own_inverse[:, None]).astype(jnp.bfloat16)
    node_output = (
        contract(hidden_one, self_two, 1, 0) + contract(agg_two, neigh_two, 1, 0)
    ).astype(jnp.bfloat16)
    down_self = contract(cotangent, self_two, 1, 1)
    neighbor_sum = contract(named_by, down_all, 0, 0)
    grad_hidden = down_self + neighbor_sum
    grad_pre = (grad_hidden * silu_slope(pre_one)).astype(jnp.bfloat16)
    terms = jnp.concatenate(
        [
            contract(own_feats, grad_pre, 1, 0),
            contract(own_agg_one, grad_pre, 1, 0),
            contract(hidden_one, cotangent, 0, 0),
            contract(agg_two, cotangent, 0, 0),
        ],
        axis=0,
    )
    with jax.named_scope("weight_grad_sum"):
        if lax.axis_size("dp") == 2 and devices == 16:
            half = terms.shape[1] // 2
            weight_grads = jnp.concatenate(
                [
                    halving_scatter(terms[:, :half], [0, 4, 1, 3, 2]),
                    halving_scatter(terms[:, half:], [0, 1, 4, 2, 3]),
                ],
                axis=1,
            )
        else:
            weight_grads = lax.psum_scatter(terms, ("dp", "mp"), scatter_dimension=0, tiled=True)
    return (node_output, weight_grads)


def solution(mesh):
    in_specs = (
        P("mp", "dp"),
        P(),
        P(),
        P("dp", None),
        P("dp", None),
        P("dp"),
        P(("dp", "mp"), None),
    )
    out_specs = (P(("dp", "mp"), None), P(("dp", "mp"), None))
    return jax.shard_map(shards, mesh=mesh, in_specs=in_specs, out_specs=out_specs, check_vma=False)
```

```python
import jax
import jax.numpy as jnp
from jax import lax
from jax.sharding import PartitionSpec as P


def column_mean(table, indices, live, inverse):
    total = jnp.zeros((table.shape[0], indices.shape[1]), jnp.float32)
    for slot_index in range(indices.shape[0]):
        picked = jnp.take(table, indices[slot_index], axis=1)
        kept = jnp.where(live[slot_index][None, :], picked, jnp.zeros_like(picked))
        total = total + kept.astype(jnp.float32)
    return (total * inverse[None, :]).astype(jnp.bfloat16)


def silu_slope(values):
    sigmoid = jax.nn.sigmoid(values)
    return sigmoid * (1.0 + values * (1.0 - sigmoid))


def contract(left, right, left_dim, right_dim):
    return lax.dot_general(
        left, right, (((left_dim,), (right_dim,)), ((), ())), preferred_element_type=jnp.float32
    )


def swap(values, axis, mask):
    size = lax.axis_size(axis)
    return lax.ppermute(values, axis, [(j, j ^ mask) for j in range(size)])


def halving_scatter(terms, order):
    n_mp = lax.axis_size("mp")
    top = n_mp.bit_length() - 1
    place = lax.axis_index("dp") * n_mp + lax.axis_index("mp")
    rows = terms.shape[0] // (2 * n_mp)
    bits = list(range(top, -1, -1))
    values = terms.reshape((2,) * (top + 1) + (rows, terms.shape[1]))
    for bit in order:
        position = bits.index(bit)
        mine = (place >> bit) & 1
        keep = lax.dynamic_index_in_dim(values, mine, position, keepdims=False)
        send = lax.dynamic_index_in_dim(values, 1 - mine, position, keepdims=False)
        got = swap(send, "dp", 1) if bit == top else swap(send, "mp", 1 << bit)
        values = keep + got
        bits.pop(position)
    return values.reshape(rows, terms.shape[1])


def doubling_step(current, order, step):
    own = lax.axis_index("mp")
    bit = order[step]
    got = swap(current, "mp", 1 << bit)
    low = jnp.where((own >> bit) & 1 == 0, current, got)
    high = jnp.where((own >> bit) & 1 == 0, got, current)
    return jnp.stack([low, high], axis=sum(1 for done in order[:step] if done > bit))


def doubling_gather(rows, order):
    current = rows
    for step in range(len(order)):
        current = doubling_step(current, order, step)
    return current.reshape(-1, rows.shape[-1])


def split_gather(rows, order, other):
    if other == order:
        return doubling_gather(rows, order)
    half = rows.shape[1] // 2
    return jnp.concatenate(
        [doubling_gather(rows[:, :half], order), doubling_gather(rows[:, half:], other)], axis=1
    )


def halving_step(state, order, step):
    values, bits, place = state
    top = lax.axis_size("mp").bit_length() - 1
    bit = order[step]
    position = bits.index(bit)
    mine = (place >> bit) & 1
    keep = lax.dynamic_index_in_dim(values, mine, position, keepdims=False)
    send = lax.dynamic_index_in_dim(values, 1 - mine, position, keepdims=False)
    got = swap(send, "dp", 1) if bit == top else swap(send, "mp", 1 << bit)
    return (keep + got, [b for b in bits if b != bit], place)


def halving_start(terms):
    n_mp = lax.axis_size("mp")
    top = n_mp.bit_length() - 1
    place = lax.axis_index("dp") * n_mp + lax.axis_index("mp")
    rows = terms.shape[0] // (2 * n_mp)
    values = terms.reshape((2,) * (top + 1) + (rows, terms.shape[1]))
    return (values, list(range(top, -1, -1)), place)


def last_block_sum(block):
    mp_index = lax.axis_index("mp")
    rows = block.shape[0] // 8
    values = block.reshape(2, 2, 2, rows, block.shape[1])
    bits = [2, 1, 0]
    for bit in [0, 1, 2]:
        position = bits.index(bit)
        mine = (mp_index >> bit) & 1
        keep = lax.dynamic_index_in_dim(values, mine, position, keepdims=False)
        send = lax.dynamic_index_in_dim(values, 1 - mine, position, keepdims=False)
        values = keep + swap(send, "mp", 1 << bit)
        bits.pop(position)
    values = values.reshape(rows, block.shape[1])
    values = values + swap(values, "mp", 8)
    values = values + swap(values, "dp", 1)
    lands = (lax.axis_index("dp") == 1) & (mp_index >= 8)
    return jnp.where(lands, values, jnp.zeros_like(values))


def shards(
    node_features, weights_one, weights_two, neighbor_owner, neighbor_row, neighbor_count, cotangent
):
    devices = lax.axis_size("mp")
    own_index = lax.axis_index("mp")
    node_dev = cotangent.shape[0]
    all_nodes = neighbor_owner.shape[0]
    fanout = neighbor_owner.shape[1]
    feat_width = weights_one.shape[0] // 2
    hidden = weights_one.shape[1]
    live = lax.broadcasted_iota(jnp.int32, (all_nodes, fanout), 1) < neighbor_count[:, None]
    inverse_all = 1.0 / neighbor_count.astype(jnp.float32)

    owner_ids = lax.broadcasted_iota(jnp.int32, (devices, 1, 1), 0)
    match = (neighbor_owner[None, :, :] == owner_ids) & live[None, :, :]
    rowsel = jnp.max(jnp.where(match, neighbor_row[None, :, :], -1), axis=2)

    self_two = weights_two[:hidden]
    neigh_two = weights_two[hidden:]
    own_inverse = lax.dynamic_slice_in_dim(inverse_all, own_index * node_dev, node_dev, 0)
    order = list(range(devices.bit_length() - 2, -1, -1))
    other = [1] + [bit for bit in order if bit != 1] if devices == 16 else order
    dense_one = all_nodes * all_nodes <= 4096 * 4096

    down_neigh = (contract(cotangent, neigh_two, 1, 1) * own_inverse[:, None]).astype(jnp.bfloat16)
    half = down_neigh.shape[1] // 2
    parts = [down_neigh[:, :half], down_neigh[:, half:]]
    orders = [order, other]
    steps_done = 0

    def advance(parts, steps_done):
        if steps_done < len(order):
            parts = [doubling_step(p, o, steps_done) for p, o in zip(parts, orders)]
        return parts, steps_done + 1

    parts, steps_done = advance(parts, steps_done)

    with jax.named_scope("layer_one_mean"):
        if dense_one:
            row_ids = lax.broadcasted_iota(jnp.int32, (1, node_dev, 1), 1)
            adjacency = (rowsel[:, None, :] == row_ids).astype(jnp.bfloat16)
            adjacency = adjacency.reshape(devices * node_dev, all_nodes)
            parts, adjacency = lax.optimization_barrier((parts, adjacency))
            parts, steps_done = advance(parts, steps_done)
            summed = contract(node_features, adjacency, 1, 0)
            agg_one_cols = (summed * inverse_all[None, :]).astype(jnp.bfloat16)
        else:
            owner_slots = neighbor_owner.T
            global_ids = owner_slots * node_dev + neighbor_row.T
            agg_one_cols = column_mean(node_features, global_ids, live.T, inverse_all)
    parts, agg_one_cols = lax.optimization_barrier((parts, agg_one_cols))
    parts, steps_done = advance(parts, steps_done)

    own_feats, own_agg_one = (
        lax.all_to_all(node_features, "mp", split_axis=1, concat_axis=0, tiled=True),
        lax.all_to_all(agg_one_cols, "mp", split_axis=1, concat_axis=0, tiled=True),
    )
    parts, own_agg_one = lax.optimization_barrier((parts, own_agg_one))
    while steps_done < len(order):
        parts, steps_done = advance(parts, steps_done)
    down_all = jnp.concatenate([p.reshape(-1, half) for p in parts], axis=1)

    with jax.named_scope("neighbor_tables"):
        row_ids = lax.broadcasted_iota(jnp.int32, (1, node_dev, 1), 1)
        own_sel = lax.dynamic_slice_in_dim(rowsel, own_index * node_dev, node_dev, 1)
        own_edges = (own_sel[:, None, :] == row_ids).astype(jnp.bfloat16)
        own_edges = own_edges.reshape(devices * node_dev, node_dev)
        mine_sel = lax.dynamic_index_in_dim(rowsel, own_index, 0, keepdims=False)
        named_by = (mine_sel[:, None] == row_ids.reshape(1, node_dev)).astype(jnp.bfloat16)

    pre_one = contract(own_feats, weights_one[:feat_width], 0, 0) + contract(
        own_agg_one, weights_one[feat_width:], 0, 0
    )
    hidden_one = jax.nn.silu(pre_one).astype(jnp.bfloat16)
    down_self = contract(cotangent, self_two, 1, 1)
    neighbor_sum = contract(named_by, down_all, 0, 0)
    grad_hidden = down_self + neighbor_sum
    grad_pre = (grad_hidden * silu_slope(pre_one)).astype(jnp.bfloat16)
    early_terms = [
        contract(own_feats, grad_pre, 1, 0),
        contract(own_agg_one, grad_pre, 1, 0),
        contract(hidden_one, cotangent, 0, 0),
    ]
    paced = lax.axis_size("dp") == 2 and devices == 16
    if paced:
        early = jnp.concatenate(early_terms + [jnp.zeros_like(early_terms[0])], axis=0)
        cols = early.shape[1] // 2
        sum_orders = [[0, 4, 1, 3, 2], [0, 1, 4, 2, 3]]
        sums = [halving_start(early[:, :cols]), halving_start(early[:, cols:])]
        hparts = [hidden_one[:, :half], hidden_one[:, half:]]
        for step in range(len(order)):
            hparts = [doubling_step(p, o, step) for p, o in zip(hparts, orders)]
            sums = [halving_step(t, o, step) for t, o in zip(sums, sum_orders)]
            hparts, sum_values = lax.optimization_barrier((hparts, [t[0] for t in sums]))
            sums = [(v, t[1], t[2]) for v, t in zip(sum_values, sums)]
        hidden_all = jnp.concatenate([p.reshape(-1, half) for p in hparts], axis=1)
    else:
        hidden_all = split_gather(hidden_one, order, other)
    total = contract(own_edges, hidden_all, 0, 0)
    agg_two = (total * own_inverse[:, None]).astype(jnp.bfloat16)
    node_output = (
        contract(hidden_one, self_two, 1, 0) + contract(agg_two, neigh_two, 1, 0)
    ).astype(jnp.bfloat16)
    last_term = contract(agg_two, cotangent, 0, 0)
    with jax.named_scope("weight_grad_sum"):
        if paced:
            for step in range(len(order), len(sum_orders[0])):
                sums = [halving_step(t, o, step) for t, o in zip(sums, sum_orders)]
            rows = sums[0][0].shape[-2]
            weight_grads = jnp.concatenate([t[0].reshape(rows, cols) for t in sums], axis=1)
            weight_grads = weight_grads + last_block_sum(last_term)
        else:
            terms = jnp.concatenate(early_terms + [last_term], axis=0)
            weight_grads = lax.psum_scatter(terms, ("dp", "mp"), scatter_dimension=0, tiled=True)
    return (node_output, weight_grads)


def solution(mesh):
    in_specs = (
        P("mp", "dp"),
        P(),
        P(),
        P("dp", None),
        P("dp", None),
        P("dp"),
        P(("dp", "mp"), None),
    )
    out_specs = (P(("dp", "mp"), None), P(("dp", "mp"), None))
    return jax.shard_map(shards, mesh=mesh, in_specs=in_specs, out_specs=out_specs, check_vma=False)
```

```python
import jax
import jax.numpy as jnp
from jax import lax
from jax.sharding import PartitionSpec as P


def column_mean(table, indices, live, inverse):
    total = jnp.zeros((table.shape[0], indices.shape[1]), jnp.float32)
    for slot_index in range(indices.shape[0]):
        picked = jnp.take(table, indices[slot_index], axis=1)
        kept = jnp.where(live[slot_index][None, :], picked, jnp.zeros_like(picked))
        total = total + kept.astype(jnp.float32)
    return (total * inverse[None, :]).astype(jnp.bfloat16)


def silu_slope(values):
    sigmoid = jax.nn.sigmoid(values)
    return sigmoid * (1.0 + values * (1.0 - sigmoid))


def contract(left, right, left_dim, right_dim):
    return lax.dot_general(
        left, right, (((left_dim,), (right_dim,)), ((), ())), preferred_element_type=jnp.float32
    )


def swap(values, axis, mask):
    size = lax.axis_size(axis)
    return lax.ppermute(values, axis, [(j, j ^ mask) for j in range(size)])


def halving_scatter(terms, order):
    n_mp = lax.axis_size("mp")
    top = n_mp.bit_length() - 1
    place = lax.axis_index("dp") * n_mp + lax.axis_index("mp")
    rows = terms.shape[0] // (2 * n_mp)
    bits = list(range(top, -1, -1))
    values = terms.reshape((2,) * (top + 1) + (rows, terms.shape[1]))
    for bit in order:
        position = bits.index(bit)
        mine = (place >> bit) & 1
        keep = lax.dynamic_index_in_dim(values, mine, position, keepdims=False)
        send = lax.dynamic_index_in_dim(values, 1 - mine, position, keepdims=False)
        got = swap(send, "dp", 1) if bit == top else swap(send, "mp", 1 << bit)
        values = keep + got
        bits.pop(position)
    return values.reshape(rows, terms.shape[1])


def doubling_step(current, order, step):
    own = lax.axis_index("mp")
    bit = order[step]
    got = swap(current, "mp", 1 << bit)
    low = jnp.where((own >> bit) & 1 == 0, current, got)
    high = jnp.where((own >> bit) & 1 == 0, got, current)
    return jnp.stack([low, high], axis=sum(1 for done in order[:step] if done > bit))


def doubling_gather(rows, order):
    current = rows
    for step in range(len(order)):
        current = doubling_step(current, order, step)
    return current.reshape(-1, rows.shape[-1])


def split_gather(rows, order, other):
    if other == order:
        return doubling_gather(rows, order)
    half = rows.shape[1] // 2
    return jnp.concatenate(
        [doubling_gather(rows[:, :half], order), doubling_gather(rows[:, half:], other)], axis=1
    )


def shards(
    node_features, weights_one, weights_two, neighbor_owner, neighbor_row, neighbor_count, cotangent
):
    devices = lax.axis_size("mp")
    own_index = lax.axis_index("mp")
    node_dev = cotangent.shape[0]
    all_nodes = neighbor_owner.shape[0]
    fanout = neighbor_owner.shape[1]
    feat_width = weights_one.shape[0] // 2
    hidden = weights_one.shape[1]
    live = lax.broadcasted_iota(jnp.int32, (all_nodes, fanout), 1) < neighbor_count[:, None]
    inverse_all = 1.0 / neighbor_count.astype(jnp.float32)

    owner_ids = lax.broadcasted_iota(jnp.int32, (devices, 1, 1), 0)
    match = (neighbor_owner[None, :, :] == owner_ids) & live[None, :, :]
    rowsel = jnp.max(jnp.where(match, neighbor_row[None, :, :], -1), axis=2)

    self_two = weights_two[:hidden]
    neigh_two = weights_two[hidden:]
    own_inverse = lax.dynamic_slice_in_dim(inverse_all, own_index * node_dev, node_dev, 0)
    order = list(range(devices.bit_length() - 2, -1, -1))
    other = [1] + [bit for bit in order if bit != 1] if devices == 16 else order
    dense_one = all_nodes * all_nodes <= 4096 * 4096

    down_neigh = (contract(cotangent, neigh_two, 1, 1) * own_inverse[:, None]).astype(jnp.bfloat16)
    half = down_neigh.shape[1] // 2
    parts = [down_neigh[:, :half], down_neigh[:, half:]]
    orders = [order, other]
    steps_done = 0

    def advance(parts, steps_done):
        if steps_done < len(order):
            parts = [doubling_step(p, o, steps_done) for p, o in zip(parts, orders)]
        return parts, steps_done + 1

    parts, steps_done = advance(parts, steps_done)

    with jax.named_scope("layer_one_mean"):
        if dense_one:
            row_ids = lax.broadcasted_iota(jnp.int32, (1, node_dev, 1), 1)
            adjacency = (rowsel[:, None, :] == row_ids).astype(jnp.bfloat16)
            adjacency = adjacency.reshape(devices * node_dev, all_nodes)
            parts, adjacency = lax.optimization_barrier((parts, adjacency))
            parts, steps_done = advance(parts, steps_done)
            summed = contract(node_features, adjacency, 1, 0)
            agg_one_cols = (summed * inverse_all[None, :]).astype(jnp.bfloat16)
        else:
            owner_slots = neighbor_owner.T
            global_ids = owner_slots * node_dev + neighbor_row.T
            agg_one_cols = column_mean(node_features, global_ids, live.T, inverse_all)
    own_feats, own_agg_one = (
        lax.all_to_all(node_features, "mp", split_axis=1, concat_axis=0, tiled=True),
        lax.all_to_all(agg_one_cols, "mp", split_axis=1, concat_axis=0, tiled=True),
    )
    parts, own_agg_one = lax.optimization_barrier((parts, own_agg_one))
    parts, steps_done = advance(parts, steps_done)
    while steps_done < len(order):
        parts, steps_done = advance(parts, steps_done)
    down_all = jnp.concatenate([p.reshape(-1, half) for p in parts], axis=1)

    with jax.named_scope("neighbor_tables"):
        row_ids = lax.broadcasted_iota(jnp.int32, (1, node_dev, 1), 1)
        own_sel = lax.dynamic_slice_in_dim(rowsel, own_index * node_dev, node_dev, 1)
        own_edges = (own_sel[:, None, :] == row_ids).astype(jnp.bfloat16)
        own_edges = own_edges.reshape(devices * node_dev, node_dev)
        mine_sel = lax.dynamic_index_in_dim(rowsel, own_index, 0, keepdims=False)
        named_by = (mine_sel[:, None] == row_ids.reshape(1, node_dev)).astype(jnp.bfloat16)

    pre_one = contract(own_feats, weights_one[:feat_width], 0, 0) + contract(
        own_agg_one, weights_one[feat_width:], 0, 0
    )
    hidden_one = jax.nn.silu(pre_one).astype(jnp.bfloat16)
    hidden_all = split_gather(hidden_one, order, other)
    total = contract(own_edges, hidden_all, 0, 0)
    agg_two = (total * own_inverse[:, None]).astype(jnp.bfloat16)
    node_output = (
        contract(hidden_one, self_two, 1, 0) + contract(agg_two, neigh_two, 1, 0)
    ).astype(jnp.bfloat16)
    down_self = contract(cotangent, self_two, 1, 1)
    neighbor_sum = contract(named_by, down_all, 0, 0)
    grad_hidden = down_self + neighbor_sum
    grad_pre = (grad_hidden * silu_slope(pre_one)).astype(jnp.bfloat16)
    terms = jnp.concatenate(
        [
            contract(own_feats, grad_pre, 1, 0),
            contract(own_agg_one, grad_pre, 1, 0),
            contract(hidden_one, cotangent, 0, 0),
            contract(agg_two, cotangent, 0, 0),
        ],
        axis=0,
    )
    with jax.named_scope("weight_grad_sum"):
        if lax.axis_size("dp") == 2 and devices == 16:
            half = terms.shape[1] // 2
            weight_grads = jnp.concatenate(
                [
                    halving_scatter(terms[:, :half], [0, 4, 1, 3, 2]),
                    halving_scatter(terms[:, half:], [0, 1, 4, 2, 3]),
                ],
                axis=1,
            )
        else:
            weight_grads = lax.psum_scatter(terms, ("dp", "mp"), scatter_dimension=0, tiled=True)
    return (node_output, weight_grads)


def solution(mesh):
    in_specs = (
        P("mp", "dp"),
        P(),
        P(),
        P("dp", None),
        P("dp", None),
        P("dp"),
        P(("dp", "mp"), None),
    )
    out_specs = (P(("dp", "mp"), None), P(("dp", "mp"), None))
    return jax.shard_map(shards, mesh=mesh, in_specs=in_specs, out_specs=out_specs, check_vma=False)
```

```python
import jax
import jax.numpy as jnp
from jax import lax
from jax.sharding import PartitionSpec as P


def column_mean(table, indices, live, inverse):
    total = jnp.zeros((table.shape[0], indices.shape[1]), jnp.float32)
    for slot_index in range(indices.shape[0]):
        picked = jnp.take(table, indices[slot_index], axis=1)
        kept = jnp.where(live[slot_index][None, :], picked, jnp.zeros_like(picked))
        total = total + kept.astype(jnp.float32)
    return (total * inverse[None, :]).astype(jnp.bfloat16)


def silu_slope(values):
    sigmoid = jax.nn.sigmoid(values)
    return sigmoid * (1.0 + values * (1.0 - sigmoid))


def contract(left, right, left_dim, right_dim):
    return lax.dot_general(
        left, right, (((left_dim,), (right_dim,)), ((), ())), preferred_element_type=jnp.float32
    )


def swap(values, axis, mask):
    size = lax.axis_size(axis)
    return lax.ppermute(values, axis, [(j, j ^ mask) for j in range(size)])


def halving_scatter(terms, order):
    n_mp = lax.axis_size("mp")
    top = n_mp.bit_length() - 1
    place = lax.axis_index("dp") * n_mp + lax.axis_index("mp")
    rows = terms.shape[0] // (2 * n_mp)
    bits = list(range(top, -1, -1))
    values = terms.reshape((2,) * (top + 1) + (rows, terms.shape[1]))
    for bit in order:
        position = bits.index(bit)
        mine = (place >> bit) & 1
        keep = lax.dynamic_index_in_dim(values, mine, position, keepdims=False)
        send = lax.dynamic_index_in_dim(values, 1 - mine, position, keepdims=False)
        got = swap(send, "dp", 1) if bit == top else swap(send, "mp", 1 << bit)
        values = keep + got
        bits.pop(position)
    return values.reshape(rows, terms.shape[1])


def doubling_step(current, order, step):
    own = lax.axis_index("mp")
    bit = order[step]
    got = swap(current, "mp", 1 << bit)
    low = jnp.where((own >> bit) & 1 == 0, current, got)
    high = jnp.where((own >> bit) & 1 == 0, got, current)
    return jnp.stack([low, high], axis=sum(1 for done in order[:step] if done > bit))


def doubling_gather(rows, order):
    current = rows
    for step in range(len(order)):
        current = doubling_step(current, order, step)
    return current.reshape(-1, rows.shape[-1])


def split_gather(rows, order, other):
    if other == order:
        return doubling_gather(rows, order)
    half = rows.shape[1] // 2
    return jnp.concatenate(
        [doubling_gather(rows[:, :half], order), doubling_gather(rows[:, half:], other)], axis=1
    )


def shards(
    node_features, weights_one, weights_two, neighbor_owner, neighbor_row, neighbor_count, cotangent
):
    devices = lax.axis_size("mp")
    own_index = lax.axis_index("mp")
    node_dev = cotangent.shape[0]
    all_nodes = neighbor_owner.shape[0]
    fanout = neighbor_owner.shape[1]
    feat_width = weights_one.shape[0] // 2
    hidden = weights_one.shape[1]
    live = lax.broadcasted_iota(jnp.int32, (all_nodes, fanout), 1) < neighbor_count[:, None]
    inverse_all = 1.0 / neighbor_count.astype(jnp.float32)

    owner_ids = lax.broadcasted_iota(jnp.int32, (devices, 1, 1), 0)
    match = (neighbor_owner[None, :, :] == owner_ids) & live[None, :, :]
    rowsel = jnp.max(jnp.where(match, neighbor_row[None, :, :], -1), axis=2)

    self_two = weights_two[:hidden]
    neigh_two = weights_two[hidden:]
    own_inverse = lax.dynamic_slice_in_dim(inverse_all, own_index * node_dev, node_dev, 0)
    order = list(range(devices.bit_length() - 2, -1, -1))
    other = [1] + [bit for bit in order if bit != 1] if devices == 16 else order
    dense_one = all_nodes * all_nodes <= 4096 * 4096

    down_neigh = (contract(cotangent, neigh_two, 1, 1) * own_inverse[:, None]).astype(jnp.bfloat16)
    half = down_neigh.shape[1] // 2
    parts = [down_neigh[:, :half], down_neigh[:, half:]]
    orders = [order, other]
    steps_done = 0

    def advance(parts, steps_done):
        if steps_done < len(order):
            parts = [doubling_step(p, o, steps_done) for p, o in zip(parts, orders)]
        return parts, steps_done + 1

    parts, steps_done = advance(parts, steps_done)

    with jax.named_scope("layer_one_mean"):
        if dense_one:
            row_ids = lax.broadcasted_iota(jnp.int32, (1, node_dev, 1), 1)
            adjacency = (rowsel[:, None, :] == row_ids).astype(jnp.bfloat16)
            adjacency = adjacency.reshape(devices * node_dev, all_nodes)
            parts, adjacency = lax.optimization_barrier((parts, adjacency))
            parts, steps_done = advance(parts, steps_done)
            summed = contract(node_features, adjacency, 1, 0)
            agg_one_cols = (summed * inverse_all[None, :]).astype(jnp.bfloat16)
        else:
            owner_slots = neighbor_owner.T
            global_ids = owner_slots * node_dev + neighbor_row.T
            agg_one_cols = column_mean(node_features, global_ids, live.T, inverse_all)
    parts, agg_one_cols = lax.optimization_barrier((parts, agg_one_cols))
    parts, steps_done = advance(parts, steps_done)

    own_feats, own_agg_one = (
        lax.all_to_all(node_features, "mp", split_axis=1, concat_axis=0, tiled=True),
        lax.all_to_all(agg_one_cols, "mp", split_axis=1, concat_axis=0, tiled=True),
    )
    parts, own_agg_one = lax.optimization_barrier((parts, own_agg_one))

    with jax.named_scope("neighbor_tables"):
        row_ids = lax.broadcasted_iota(jnp.int32, (1, node_dev, 1), 1)
        own_sel = lax.dynamic_slice_in_dim(rowsel, own_index * node_dev, node_dev, 1)
        own_edges = (own_sel[:, None, :] == row_ids).astype(jnp.bfloat16)
        own_edges = own_edges.reshape(devices * node_dev, node_dev)
        mine_sel = lax.dynamic_index_in_dim(rowsel, own_index, 0, keepdims=False)
        named_by = (mine_sel[:, None] == row_ids.reshape(1, node_dev)).astype(jnp.bfloat16)

    pre_one = contract(own_feats, weights_one[:feat_width], 0, 0) + contract(
        own_agg_one, weights_one[feat_width:], 0, 0
    )
    hidden_one = jax.nn.silu(pre_one).astype(jnp.bfloat16)
    hparts = [hidden_one[:, :half], hidden_one[:, half:]]
    hparts = [doubling_step(p, o, 0) for p, o in zip(hparts, orders)]
    hparts, parts = lax.optimization_barrier((hparts, parts))
    while steps_done < len(order):
        parts, steps_done = advance(parts, steps_done)
    for step in range(1, len(order)):
        hparts = [doubling_step(p, o, step) for p, o in zip(hparts, orders)]
    hidden_all = jnp.concatenate([p.reshape(-1, half) for p in hparts], axis=1)
    down_all = jnp.concatenate([p.reshape(-1, half) for p in parts], axis=1)
    total = contract(own_edges, hidden_all, 0, 0)
    agg_two = (total * own_inverse[:, None]).astype(jnp.bfloat16)
    node_output = (
        contract(hidden_one, self_two, 1, 0) + contract(agg_two, neigh_two, 1, 0)
    ).astype(jnp.bfloat16)
    down_self = contract(cotangent, self_two, 1, 1)
    neighbor_sum = contract(named_by, down_all, 0, 0)
    grad_hidden = down_self + neighbor_sum
    grad_pre = (grad_hidden * silu_slope(pre_one)).astype(jnp.bfloat16)
    terms = jnp.concatenate(
        [
            contract(own_feats, grad_pre, 1, 0),
            contract(own_agg_one, grad_pre, 1, 0),
            contract(hidden_one, cotangent, 0, 0),
            contract(agg_two, cotangent, 0, 0),
        ],
        axis=0,
    )
    with jax.named_scope("weight_grad_sum"):
        if lax.axis_size("dp") == 2 and devices == 16:
            half = terms.shape[1] // 2
            weight_grads = jnp.concatenate(
                [
                    halving_scatter(terms[:, :half], [0, 4, 1, 3, 2]),
                    halving_scatter(terms[:, half:], [0, 1, 4, 2, 3]),
                ],
                axis=1,
            )
        else:
            weight_grads = lax.psum_scatter(terms, ("dp", "mp"), scatter_dimension=0, tiled=True)
    return (node_output, weight_grads)


def solution(mesh):
    in_specs = (
        P("mp", "dp"),
        P(),
        P(),
        P("dp", None),
        P("dp", None),
        P("dp"),
        P(("dp", "mp"), None),
    )
    out_specs = (P(("dp", "mp"), None), P(("dp", "mp"), None))
    return jax.shard_map(shards, mesh=mesh, in_specs=in_specs, out_specs=out_specs, check_vma=False)
```

```python
import jax
import jax.numpy as jnp
from jax import lax
from jax.sharding import PartitionSpec as P


def column_mean(table, indices, live, inverse):
    total = jnp.zeros((table.shape[0], indices.shape[1]), jnp.float32)
    for slot_index in range(indices.shape[0]):
        picked = jnp.take(table, indices[slot_index], axis=1)
        kept = jnp.where(live[slot_index][None, :], picked, jnp.zeros_like(picked))
        total = total + kept.astype(jnp.float32)
    return (total * inverse[None, :]).astype(jnp.bfloat16)


def silu_slope(values):
    sigmoid = jax.nn.sigmoid(values)
    return sigmoid * (1.0 + values * (1.0 - sigmoid))


def contract(left, right, left_dim, right_dim):
    return lax.dot_general(
        left, right, (((left_dim,), (right_dim,)), ((), ())), preferred_element_type=jnp.float32
    )


def swap(values, axis, mask):
    size = lax.axis_size(axis)
    return lax.ppermute(values, axis, [(j, j ^ mask) for j in range(size)])


def halving_scatter(terms, order):
    n_mp = lax.axis_size("mp")
    top = n_mp.bit_length() - 1
    place = lax.axis_index("dp") * n_mp + lax.axis_index("mp")
    rows = terms.shape[0] // (2 * n_mp)
    bits = list(range(top, -1, -1))
    values = terms.reshape((2,) * (top + 1) + (rows, terms.shape[1]))
    for bit in order:
        position = bits.index(bit)
        mine = (place >> bit) & 1
        keep = lax.dynamic_index_in_dim(values, mine, position, keepdims=False)
        send = lax.dynamic_index_in_dim(values, 1 - mine, position, keepdims=False)
        got = swap(send, "dp", 1) if bit == top else swap(send, "mp", 1 << bit)
        values = keep + got
        bits.pop(position)
    return values.reshape(rows, terms.shape[1])


def doubling_step(current, order, step):
    own = lax.axis_index("mp")
    bit = order[step]
    got = swap(current, "mp", 1 << bit)
    low = jnp.where((own >> bit) & 1 == 0, current, got)
    high = jnp.where((own >> bit) & 1 == 0, got, current)
    return jnp.stack([low, high], axis=sum(1 for done in order[:step] if done > bit))


def doubling_gather(rows, order):
    current = rows
    for step in range(len(order)):
        current = doubling_step(current, order, step)
    return current.reshape(-1, rows.shape[-1])


def split_gather(rows, order, other):
    if other == order:
        return doubling_gather(rows, order)
    half = rows.shape[1] // 2
    return jnp.concatenate(
        [doubling_gather(rows[:, :half], order), doubling_gather(rows[:, half:], other)], axis=1
    )


def shards(
    node_features, weights_one, weights_two, neighbor_owner, neighbor_row, neighbor_count, cotangent
):
    devices = lax.axis_size("mp")
    own_index = lax.axis_index("mp")
    node_dev = cotangent.shape[0]
    all_nodes = neighbor_owner.shape[0]
    fanout = neighbor_owner.shape[1]
    feat_width = weights_one.shape[0] // 2
    hidden = weights_one.shape[1]
    live = lax.broadcasted_iota(jnp.int32, (all_nodes, fanout), 1) < neighbor_count[:, None]
    inverse_all = 1.0 / neighbor_count.astype(jnp.float32)

    owner_ids = lax.broadcasted_iota(jnp.int32, (devices, 1, 1), 0)
    match = (neighbor_owner[None, :, :] == owner_ids) & live[None, :, :]
    rowsel = jnp.max(jnp.where(match, neighbor_row[None, :, :], -1), axis=2)

    self_two = weights_two[:hidden]
    neigh_two = weights_two[hidden:]
    own_inverse = lax.dynamic_slice_in_dim(inverse_all, own_index * node_dev, node_dev, 0)
    order = list(range(devices.bit_length() - 2, -1, -1))
    other = [1] + [bit for bit in order if bit != 1] if devices == 16 else order
    dense_one = all_nodes * all_nodes <= 4096 * 4096

    down_neigh = (contract(cotangent, neigh_two, 1, 1) * own_inverse[:, None]).astype(jnp.bfloat16)
    half = down_neigh.shape[1] // 2
    parts = [down_neigh[:, :half], down_neigh[:, half:]]
    orders = [order, other]
    steps_done = 0

    def advance(parts, steps_done):
        if steps_done < len(order):
            parts = [doubling_step(p, o, steps_done) for p, o in zip(parts, orders)]
        return parts, steps_done + 1

    parts, steps_done = advance(parts, steps_done)

    with jax.named_scope("layer_one_mean"):
        if dense_one:
            row_ids = lax.broadcasted_iota(jnp.int32, (1, node_dev, 1), 1)
            adjacency = (rowsel[:, None, :] == row_ids).astype(jnp.bfloat16)
            adjacency = adjacency.reshape(devices * node_dev, all_nodes)
            parts, adjacency = lax.optimization_barrier((parts, adjacency))
            parts, steps_done = advance(parts, steps_done)
            summed = contract(node_features, adjacency, 1, 0)
            agg_one_cols = (summed * inverse_all[None, :]).astype(jnp.bfloat16)
        else:
            owner_slots = neighbor_owner.T
            global_ids = owner_slots * node_dev + neighbor_row.T
            agg_one_cols = column_mean(node_features, global_ids, live.T, inverse_all)
    parts, agg_one_cols = lax.optimization_barrier((parts, agg_one_cols))
    parts, steps_done = advance(parts, steps_done)

    own_feats, own_agg_one = (
        lax.all_to_all(node_features, "mp", split_axis=1, concat_axis=0, tiled=True),
        lax.all_to_all(agg_one_cols, "mp", split_axis=1, concat_axis=0, tiled=True),
    )
    parts, own_agg_one = lax.optimization_barrier((parts, own_agg_one))

    with jax.named_scope("neighbor_tables"):
        row_ids = lax.broadcasted_iota(jnp.int32, (1, node_dev, 1), 1)
        own_sel = lax.dynamic_slice_in_dim(rowsel, own_index * node_dev, node_dev, 1)
        own_edges = (own_sel[:, None, :] == row_ids).astype(jnp.bfloat16)
        own_edges = own_edges.reshape(devices * node_dev, node_dev)
        mine_sel = lax.dynamic_index_in_dim(rowsel, own_index, 0, keepdims=False)
        named_by = (mine_sel[:, None] == row_ids.reshape(1, node_dev)).astype(jnp.bfloat16)

    pre_one = contract(own_feats, weights_one[:feat_width], 0, 0) + contract(
        own_agg_one, weights_one[feat_width:], 0, 0
    )
    hidden_one = jax.nn.silu(pre_one).astype(jnp.bfloat16)
    hparts = [hidden_one[:, :half], hidden_one[:, half:]]
    lead = 2 if devices == 16 else 1
    for step in range(lead):
        hparts = [doubling_step(p, o, step) for p, o in zip(hparts, orders)]
    hparts, parts = lax.optimization_barrier((hparts, parts))
    while steps_done < len(order):
        parts, steps_done = advance(parts, steps_done)
    for step in range(lead, len(order)):
        hparts = [doubling_step(p, o, step) for p, o in zip(hparts, orders)]
    hidden_all = jnp.concatenate([p.reshape(-1, half) for p in hparts], axis=1)
    down_all = jnp.concatenate([p.reshape(-1, half) for p in parts], axis=1)
    total = contract(own_edges, hidden_all, 0, 0)
    agg_two = (total * own_inverse[:, None]).astype(jnp.bfloat16)
    node_output = (
        contract(hidden_one, self_two, 1, 0) + contract(agg_two, neigh_two, 1, 0)
    ).astype(jnp.bfloat16)
    down_self = contract(cotangent, self_two, 1, 1)
    neighbor_sum = contract(named_by, down_all, 0, 0)
    grad_hidden = down_self + neighbor_sum
    grad_pre = (grad_hidden * silu_slope(pre_one)).astype(jnp.bfloat16)
    terms = jnp.concatenate(
        [
            contract(own_feats, grad_pre, 1, 0),
            contract(own_agg_one, grad_pre, 1, 0),
            contract(hidden_one, cotangent, 0, 0),
            contract(agg_two, cotangent, 0, 0),
        ],
        axis=0,
    )
    with jax.named_scope("weight_grad_sum"):
        if lax.axis_size("dp") == 2 and devices == 16:
            half = terms.shape[1] // 2
            weight_grads = jnp.concatenate(
                [
                    halving_scatter(terms[:, :half], [0, 4, 1, 3, 2]),
                    halving_scatter(terms[:, half:], [0, 1, 4, 2, 3]),
                ],
                axis=1,
            )
        else:
            weight_grads = lax.psum_scatter(terms, ("dp", "mp"), scatter_dimension=0, tiled=True)
    return (node_output, weight_grads)


def solution(mesh):
    in_specs = (
        P("mp", "dp"),
        P(),
        P(),
        P("dp", None),
        P("dp", None),
        P("dp"),
        P(("dp", "mp"), None),
    )
    out_specs = (P(("dp", "mp"), None), P(("dp", "mp"), None))
    return jax.shard_map(shards, mesh=mesh, in_specs=in_specs, out_specs=out_specs, check_vma=False)
```

```python
import jax
import jax.numpy as jnp
from jax import lax
from jax.sharding import PartitionSpec as P


def column_mean(table, indices, live, inverse):
    total = jnp.zeros((table.shape[0], indices.shape[1]), jnp.float32)
    for slot_index in range(indices.shape[0]):
        picked = jnp.take(table, indices[slot_index], axis=1)
        kept = jnp.where(live[slot_index][None, :], picked, jnp.zeros_like(picked))
        total = total + kept.astype(jnp.float32)
    return (total * inverse[None, :]).astype(jnp.bfloat16)


def silu_slope(values):
    sigmoid = jax.nn.sigmoid(values)
    return sigmoid * (1.0 + values * (1.0 - sigmoid))


def contract(left, right, left_dim, right_dim):
    return lax.dot_general(
        left, right, (((left_dim,), (right_dim,)), ((), ())), preferred_element_type=jnp.float32
    )


def swap(values, axis, mask):
    size = lax.axis_size(axis)
    return lax.ppermute(values, axis, [(j, j ^ mask) for j in range(size)])


def halving_scatter(terms, order):
    n_mp = lax.axis_size("mp")
    top = n_mp.bit_length() - 1
    place = lax.axis_index("dp") * n_mp + lax.axis_index("mp")
    rows = terms.shape[0] // (2 * n_mp)
    bits = list(range(top, -1, -1))
    values = terms.reshape((2,) * (top + 1) + (rows, terms.shape[1]))
    for bit in order:
        position = bits.index(bit)
        mine = (place >> bit) & 1
        keep = lax.dynamic_index_in_dim(values, mine, position, keepdims=False)
        send = lax.dynamic_index_in_dim(values, 1 - mine, position, keepdims=False)
        got = swap(send, "dp", 1) if bit == top else swap(send, "mp", 1 << bit)
        values = keep + got
        bits.pop(position)
    return values.reshape(rows, terms.shape[1])


def doubling_step(current, order, step):
    own = lax.axis_index("mp")
    bit = order[step]
    got = swap(current, "mp", 1 << bit)
    low = jnp.where((own >> bit) & 1 == 0, current, got)
    high = jnp.where((own >> bit) & 1 == 0, got, current)
    return jnp.stack([low, high], axis=sum(1 for done in order[:step] if done > bit))


def doubling_gather(rows, order):
    current = rows
    for step in range(len(order)):
        current = doubling_step(current, order, step)
    return current.reshape(-1, rows.shape[-1])


def split_gather(rows, order, other):
    if other == order:
        return doubling_gather(rows, order)
    half = rows.shape[1] // 2
    return jnp.concatenate(
        [doubling_gather(rows[:, :half], order), doubling_gather(rows[:, half:], other)], axis=1
    )


def shards(
    node_features, weights_one, weights_two, neighbor_owner, neighbor_row, neighbor_count, cotangent
):
    devices = lax.axis_size("mp")
    own_index = lax.axis_index("mp")
    node_dev = cotangent.shape[0]
    all_nodes = neighbor_owner.shape[0]
    fanout = neighbor_owner.shape[1]
    feat_width = weights_one.shape[0] // 2
    hidden = weights_one.shape[1]
    live = lax.broadcasted_iota(jnp.int32, (all_nodes, fanout), 1) < neighbor_count[:, None]
    inverse_all = 1.0 / neighbor_count.astype(jnp.float32)

    owner_ids = lax.broadcasted_iota(jnp.int32, (devices, 1, 1), 0)
    match = (neighbor_owner[None, :, :] == owner_ids) & live[None, :, :]
    rowsel = jnp.max(jnp.where(match, neighbor_row[None, :, :], -1), axis=2)

    self_two = weights_two[:hidden]
    neigh_two = weights_two[hidden:]
    own_inverse = lax.dynamic_slice_in_dim(inverse_all, own_index * node_dev, node_dev, 0)
    order = list(range(devices.bit_length() - 2, -1, -1))
    other = [1] + [bit for bit in order if bit != 1] if devices == 16 else order
    dense_one = all_nodes * all_nodes <= 4096 * 4096

    down_neigh = (contract(cotangent, neigh_two, 1, 1) * own_inverse[:, None]).astype(jnp.bfloat16)
    half = down_neigh.shape[1] // 2
    parts = [down_neigh[:, :half], down_neigh[:, half:]]
    orders = [order, other]
    steps_done = 0

    def advance(parts, steps_done):
        if steps_done < len(order):
            parts = [doubling_step(p, o, steps_done) for p, o in zip(parts, orders)]
        return parts, steps_done + 1

    parts, steps_done = advance(parts, steps_done)

    with jax.named_scope("layer_one_mean"):
        if dense_one:
            row_ids = lax.broadcasted_iota(jnp.int32, (1, node_dev, 1), 1)
            adjacency = (rowsel[:, None, :] == row_ids).astype(jnp.bfloat16)
            adjacency = adjacency.reshape(devices * node_dev, all_nodes)
            parts, adjacency = lax.optimization_barrier((parts, adjacency))
            parts, steps_done = advance(parts, steps_done)
            summed = contract(node_features, adjacency, 1, 0)
            agg_one_cols = (summed * inverse_all[None, :]).astype(jnp.bfloat16)
        else:
            owner_slots = neighbor_owner.T
            global_ids = owner_slots * node_dev + neighbor_row.T
            agg_one_cols = column_mean(node_features, global_ids, live.T, inverse_all)
    parts, agg_one_cols = lax.optimization_barrier((parts, agg_one_cols))
    if devices != 16:
        parts, steps_done = advance(parts, steps_done)

    own_feats, own_agg_one = (
        lax.all_to_all(node_features, "mp", split_axis=1, concat_axis=0, tiled=True),
        lax.all_to_all(agg_one_cols, "mp", split_axis=1, concat_axis=0, tiled=True),
    )
    parts, own_agg_one = lax.optimization_barrier((parts, own_agg_one))

    with jax.named_scope("neighbor_tables"):
        row_ids = lax.broadcasted_iota(jnp.int32, (1, node_dev, 1), 1)
        own_sel = lax.dynamic_slice_in_dim(rowsel, own_index * node_dev, node_dev, 1)
        own_edges = (own_sel[:, None, :] == row_ids).astype(jnp.bfloat16)
        own_edges = own_edges.reshape(devices * node_dev, node_dev)
        mine_sel = lax.dynamic_index_in_dim(rowsel, own_index, 0, keepdims=False)
        named_by = (mine_sel[:, None] == row_ids.reshape(1, node_dev)).astype(jnp.bfloat16)

    pre_one = contract(own_feats, weights_one[:feat_width], 0, 0) + contract(
        own_agg_one, weights_one[feat_width:], 0, 0
    )
    hidden_one = jax.nn.silu(pre_one).astype(jnp.bfloat16)
    hparts = [hidden_one[:, :half], hidden_one[:, half:]]
    hparts = [doubling_step(p, o, 0) for p, o in zip(hparts, orders)]
    hparts, parts = lax.optimization_barrier((hparts, parts))
    while steps_done < len(order):
        parts, steps_done = advance(parts, steps_done)
    for step in range(1, len(order)):
        hparts = [doubling_step(p, o, step) for p, o in zip(hparts, orders)]
    hidden_all = jnp.concatenate([p.reshape(-1, half) for p in hparts], axis=1)
    down_all = jnp.concatenate([p.reshape(-1, half) for p in parts], axis=1)
    total = contract(own_edges, hidden_all, 0, 0)
    agg_two = (total * own_inverse[:, None]).astype(jnp.bfloat16)
    node_output = (
        contract(hidden_one, self_two, 1, 0) + contract(agg_two, neigh_two, 1, 0)
    ).astype(jnp.bfloat16)
    down_self = contract(cotangent, self_two, 1, 1)
    neighbor_sum = contract(named_by, down_all, 0, 0)
    grad_hidden = down_self + neighbor_sum
    grad_pre = (grad_hidden * silu_slope(pre_one)).astype(jnp.bfloat16)
    terms = jnp.concatenate(
        [
            contract(own_feats, grad_pre, 1, 0),
            contract(own_agg_one, grad_pre, 1, 0),
            contract(hidden_one, cotangent, 0, 0),
            contract(agg_two, cotangent, 0, 0),
        ],
        axis=0,
    )
    with jax.named_scope("weight_grad_sum"):
        if lax.axis_size("dp") == 2 and devices == 16:
            half = terms.shape[1] // 2
            weight_grads = jnp.concatenate(
                [
                    halving_scatter(terms[:, :half], [0, 4, 1, 3, 2]),
                    halving_scatter(terms[:, half:], [0, 1, 4, 2, 3]),
                ],
                axis=1,
            )
        else:
            weight_grads = lax.psum_scatter(terms, ("dp", "mp"), scatter_dimension=0, tiled=True)
    return (node_output, weight_grads)


def solution(mesh):
    in_specs = (
        P("mp", "dp"),
        P(),
        P(),
        P("dp", None),
        P("dp", None),
        P("dp"),
        P(("dp", "mp"), None),
    )
    out_specs = (P(("dp", "mp"), None), P(("dp", "mp"), None))
    return jax.shard_map(shards, mesh=mesh, in_specs=in_specs, out_specs=out_specs, check_vma=False)
```
